512 devices in a mesh: grp: 4 (over x), ch: 128 (over y, z, core).
Axes of the slice: x: 4, y: 4, z: 16, core: 2. Of those that a mesh axis runs over, the one named last changes fastest.
Arguments:
- raw_strain: bfloat16 [4, 7680, 8192], P('grp', 'ch'), may hold values from -6 to 6
- window_valid: int32 [4, 8192], P(None, 'ch'), may hold values 0 or 1
- band_first: int32 [8192], P('ch'), may hold values from 1 to 17
- band_end: int32 [8192], P('ch'), may hold values from 34 to 128
Outputs:
- stacked: float32 [8192, 32, 128], P('ch')
The draws below stay inside these ranges and needn't reach their ends.
All inputs are finite; a program needn't handle non-finite values. No bound on the sum of `window_valid` on one device may be relied on, other than what follows from the above.
Results may differ from the reference program's by a relative error of at most 0.008.
Values may be sent and summed in bfloat16 or wider, within the bound.
No kernel may reach another device: no remote copies, remote signals or barrier semaphores. Data moves between devices by JAX's collectives and lax.ppermute only.
A program may use at most 64 MiB of HBM per device.

```python
import jax
import jax.numpy as jnp
from jax import lax

CH_DEV = 64
NT = 7680
F = 384
KH = 128
SMOOTH = 65
LAGS = 32
LAG_STEP = 10
WINDOWS = 4
CHANNELS = 8192


def set_ends(values, stream_key, low, top_value):
    place = [jax.random.randint(jax.random.fold_in(stream_key, axis), (), 0, length) for axis, length in enumerate(values.shape)]
    widest = values.shape.index(max(values.shape))
    next_to = place[:widest] + [(place[widest] + 1) % values.shape[widest]] + place[widest + 1:]
    return values.at[tuple(place)].set(low).at[tuple(next_to)].set(top_value)


def block_scale(rng, extent, shards, least, high):
    gain = 1.0
    for position, shards_of in shards:
        draws = jax.random.uniform(jax.random.fold_in(jax.random.fold_in(rng, 6), position), (shards_of,), jnp.float32, least / len(shards), high / len(shards))
        gain = gain * jnp.repeat(jnp.exp(draws), extent[position] // shards_of).reshape((-1,) + (1,) * (len(extent) - 1 - position))
    return gain


def bell_draw(key, dims, deviation, reach, cuts=(), kind=jnp.bfloat16):
    array = jax.random.normal(key, dims, jnp.float32) * deviation
    if len(cuts) > 0:
        array = block_scale(key, dims, cuts, -0.22, 0.18) * array
    return jnp.clip(array, min=-reach, max=reach).astype(kind)


def setup_inputs(seed: int = 0) -> dict:
    splits = jax.random.split(jax.random.key(seed), 5)
    raw_strain = bell_draw(splits[0], (WINDOWS, NT, CHANNELS), 1.0, 6.0, ((0, 4), (1, 128)))
    window_valid = set_ends((jax.random.randint(splits[1], (WINDOWS, CHANNELS), 0, 4) < 3).astype(jnp.int32), jax.random.fold_in(splits[1], 1), 0, 1)
    band_first = set_ends(jax.random.randint(splits[2], (CHANNELS,), 1, KH // 8 + 2), jax.random.fold_in(splits[2], 1), 1, (KH // 8 + 2) - 1).astype(jnp.int32)
    band_end = set_ends(jax.random.randint(splits[3], (CHANNELS,), KH // 4 + 2, KH + 1), jax.random.fold_in(splits[3], 1), KH // 4 + 2, KH).astype(jnp.int32)
    return dict(raw_strain=raw_strain, window_valid=window_valid, band_first=band_first, band_end=band_end)


eps_white = 1e-06

def dft_matrix(samples, bin_count):
    sample_index = jnp.arange(samples, dtype=jnp.int32)[:, None]
    orders = jnp.arange(1, bin_count + 1, dtype=jnp.int32)[None, :]
    phases = (sample_index * orders % samples).astype(jnp.float32) * (2.0 * jnp.pi / samples)
    return jnp.concatenate([jnp.cos(phases), -jnp.sin(phases)], axis=1).astype(jnp.bfloat16)

def smoothing_matrix(bin_count, window_bins):
    row_index = jnp.arange(bin_count, dtype=jnp.int32)[:, None]
    col_index = jnp.arange(bin_count, dtype=jnp.int32)[None, :]
    distance = (row_index - col_index) % bin_count
    halfwidth = window_bins // 2
    inside = (distance <= halfwidth) | (distance >= bin_count - halfwidth)
    return inside.astype(jnp.float32)

def whiten(spectra, bin_count, window_bins):
    real_part = spectra[..., :bin_count]
    imag_part = spectra[..., bin_count:]
    magnitude = jnp.sqrt(real_part * real_part + imag_part * imag_part)
    averaged = jnp.dot(magnitude, smoothing_matrix(bin_count, window_bins), precision=lax.Precision.HIGHEST, preferred_element_type=jnp.float32) / window_bins
    factor = 1.0 / (averaged + eps_white)
    return (spectra * jnp.concatenate([factor, factor], axis=-1)).astype(jnp.bfloat16)

def rotated(extended, lag_first, lag_count, lag_step, samples, bin_count):
    orders = jnp.arange(1, bin_count + 1, dtype=jnp.int32)[None, :]
    shifts = ((lag_first + jnp.arange(lag_count, dtype=jnp.int32)) * lag_step)[:, None]
    phases = (shifts * orders % samples).astype(jnp.float32) * (2.0 * jnp.pi / samples)
    cosine = jnp.cos(phases)
    sine_part = jnp.sin(phases)
    real_part = extended[..., :bin_count].astype(jnp.float32)[:, :, None, :]
    imag_part = extended[..., bin_count:].astype(jnp.float32)[:, :, None, :]
    rotated_real = real_part * cosine + imag_part * sine_part
    rotated_imag = imag_part * cosine - real_part * sine_part
    return jnp.concatenate([rotated_real, rotated_imag], axis=-1).astype(jnp.bfloat16)

def diagonal_band(matrix, offsets):
    row_count, col_count = matrix.shape
    flat_rows = matrix.reshape(row_count * col_count)
    padded = jnp.concatenate([flat_rows, jnp.zeros((row_count,), matrix.dtype)])
    skewed = padded.reshape(row_count, col_count + 1)
    return skewed[:, :offsets]

def lag_band(block_full, offsets):
    banded = jax.vmap(lambda matrix: diagonal_band(matrix, offsets))(block_full)
    return jnp.transpose(banded, (1, 0, 2))

def normalise(lagged, pair_counts, band_lows, band_highs, bin_count):
    offsets = jnp.arange(lagged.shape[2], dtype=jnp.int32)[None, :]
    in_band = (offsets >= band_lows[:, None]) & (offsets < band_highs[:, None])
    weights = jnp.where(in_band, 1.0 / jnp.sqrt(float(bin_count) * jnp.maximum(pair_counts, 1.0)), 0.0)
    return lagged * weights[:, None, :]

def reference(raw_strain, window_valid, band_first, band_end):
    dft_table = dft_matrix(NT, F).astype(jnp.float32)

    def transform(samples_block):
        spectra = lax.dot_general(samples_block.astype(jnp.float32), dft_table, (((0,), (0,)), ((), ())), precision=lax.Precision.HIGHEST, preferred_element_type=jnp.float32)
        return whiten(spectra, F, SMOOTH)
    whitened = lax.map(transform, raw_strain)
    valid_flags = window_valid.astype(jnp.bfloat16)
    whitened = whitened * valid_flags[:, :, None]
    blocks_up = (KH + CH_DEV - 1) // CH_DEV
    reach_rows = CH_DEV * (blocks_up + 1)
    padded_white = jnp.concatenate([whitened, jnp.zeros((WINDOWS, blocks_up * CH_DEV, 2 * F), jnp.bfloat16)], axis=1)
    padded_flags = jnp.concatenate([valid_flags, jnp.zeros((WINDOWS, blocks_up * CH_DEV), jnp.bfloat16)], axis=1)

    def one_block(block_index):
        block_start = (block_index * CH_DEV).astype(jnp.int32)
        extended = lax.dynamic_slice_in_dim(padded_white, block_start, reach_rows, 1)
        ext_flags = lax.dynamic_slice_in_dim(padded_flags, block_start, reach_rows, 1)
        own_rows = extended[:, :CH_DEV]
        turned = rotated(extended, -(LAGS // 2), LAGS, LAG_STEP, NT, F)
        block_full = jnp.einsum('nak,nblk->lab', own_rows.astype(jnp.float32), turned.astype(jnp.float32), precision=lax.Precision.HIGHEST, preferred_element_type=jnp.float32)
        lagged = lag_band(block_full, KH)
        pair_full = jnp.einsum('na,nb->ab', ext_flags[:, :CH_DEV].astype(jnp.float32), ext_flags.astype(jnp.float32), precision=lax.Precision.HIGHEST, preferred_element_type=jnp.float32)
        pair_counts = diagonal_band(pair_full, KH)
        band_lows = lax.dynamic_slice_in_dim(band_first, block_start, CH_DEV)
        band_highs = lax.dynamic_slice_in_dim(band_end, block_start, CH_DEV)
        return normalise(lagged, pair_counts, band_lows, band_highs, F)
    stacked = lax.map(one_block, jnp.arange(CHANNELS // CH_DEV, dtype=jnp.int32))
    return stacked.reshape(CHANNELS, LAGS, KH)
```

```python
import jax
import jax.numpy as jnp
from jax import lax
from jax.sharding import PartitionSpec as P

NT = 7680
F = 384
KH = 128
SMOOTH = 65
LAGS = 32
LAG_STEP = 10


eps_white = 1e-06


def from_behind(array, axis, by):
    count = lax.axis_size(axis)
    pairs = [(i, i + by) for i in range(count) if 0 <= i + by < count]
    return lax.ppermute(array, axis, pairs)


def smoothing_matrix(bin_count, window_bins):
    row_index = jnp.arange(bin_count, dtype=jnp.int32)[:, None]
    col_index = jnp.arange(bin_count, dtype=jnp.int32)[None, :]
    distance = (row_index - col_index) % bin_count
    halfwidth = window_bins // 2
    inside = (distance <= halfwidth) | (distance >= bin_count - halfwidth)
    return inside.astype(jnp.float32)


def whiten(spectra, bin_count, window_bins):
    real_part = spectra[..., :bin_count]
    imag_part = spectra[..., bin_count:]
    magnitude = jnp.sqrt(real_part * real_part + imag_part * imag_part)
    averaged = (
        jnp.dot(
            magnitude,
            smoothing_matrix(bin_count, window_bins),
            precision=lax.Precision.HIGHEST,
            preferred_element_type=jnp.float32,
        )
        / window_bins
    )
    factor = 1.0 / (averaged + eps_white)
    return (spectra * jnp.concatenate([factor, factor], axis=-1)).astype(jnp.bfloat16)


def phase_of(index, samples):
    return (index % samples).astype(jnp.float32) * (2.0 * jnp.pi / samples)


def dft_rows(block_starts, offsets, samples, bin_count):
    orders = jnp.arange(1, bin_count + 1, dtype=jnp.int32)[None, :]
    outer = phase_of(block_starts[:, None] * orders, samples)
    inner = phase_of(offsets[:, None] * orders, samples)
    outer_cos, outer_sin = jnp.cos(outer)[:, None, :], jnp.sin(outer)[:, None, :]
    inner_cos, inner_sin = jnp.cos(inner)[None, :, :], jnp.sin(inner)[None, :, :]
    cosine = outer_cos * inner_cos - outer_sin * inner_sin
    sine_part = outer_sin * inner_cos + outer_cos * inner_sin
    table = jnp.concatenate([cosine, -sine_part], axis=-1)
    return table.reshape(-1, 2 * bin_count).astype(jnp.bfloat16)


def unturned(own, lag_first, lag_count, lag_step, samples, bin_count):
    orders = jnp.arange(1, bin_count + 1, dtype=jnp.int32)[None, :]
    shifts = ((lag_first + jnp.arange(lag_count, dtype=jnp.int32)) * lag_step)[:, None]
    phases = (shifts * orders % samples).astype(jnp.float32) * (2.0 * jnp.pi / samples)
    cosine = jnp.cos(phases)
    sine_part = jnp.sin(phases)
    real_part = own[..., :bin_count].astype(jnp.float32)[..., None, :]
    imag_part = own[..., bin_count:].astype(jnp.float32)[..., None, :]
    back_real = real_part * cosine - imag_part * sine_part
    back_imag = imag_part * cosine + real_part * sine_part
    return jnp.concatenate([back_real, back_imag], axis=-1).astype(jnp.bfloat16)


def diagonal_band(matrix, offsets):
    row_count, col_count = matrix.shape
    flat_rows = matrix.reshape(row_count * col_count)
    padded = jnp.concatenate([flat_rows, jnp.zeros((row_count,), matrix.dtype)])
    skewed = padded.reshape(row_count, col_count + 1)
    return skewed[:, :offsets]


def lag_band(block, offsets):
    rows, lags, cols = block.shape
    flat_rows = block.reshape(rows * lags * cols)
    padded = jnp.concatenate([flat_rows, jnp.zeros((rows,), block.dtype)])
    skewed = padded.reshape(rows, lags * cols + 1)[:, : lags * cols]
    return skewed.reshape(rows, lags, cols)[:, :, :offsets]


def normalise(lagged, pair_counts, band_lows, band_highs, bin_count):
    offsets = jnp.arange(lagged.shape[2], dtype=jnp.int32)[None, :]
    in_band = (offsets >= band_lows[:, None]) & (offsets < band_highs[:, None])
    weights = jnp.where(
        in_band, 1.0 / jnp.sqrt(float(bin_count) * jnp.maximum(pair_counts, 1.0)), 0.0
    )
    return lagged * weights[:, None, :]


def local(raw_strain, window_valid, band_first, band_end):
    n_ch = lax.axis_size("ch")
    n_grp = lax.axis_size("grp")
    _, t_here, channels = raw_strain.shape
    per_dev = channels // n_ch
    pair_width = 2 * per_dev
    half = ((t_here + 1) // 2 + 15) // 16 * 16
    me = lax.axis_index("ch")
    side = me % 2

    samples = jnp.pad(raw_strain[0], ((0, 2 * half - t_here), (0, 0)))
    samples = samples.reshape(2, half, n_ch // 2, pair_width).transpose(2, 0, 1, 3)
    samples = samples.reshape(n_ch, half, pair_width)
    samples = lax.all_to_all(samples, "ch", 0, 0, tiled=True)
    samples = samples.reshape(n_ch * half, pair_width)

    block_starts = jnp.arange(n_ch, dtype=jnp.int32) * t_here
    offsets = side * half + jnp.arange(half, dtype=jnp.int32)
    table = dft_rows(block_starts, offsets, NT, F)
    partial = jnp.einsum("tc,tf->cf", samples, table, preferred_element_type=jnp.float32)
    mine = lax.dynamic_slice_in_dim(partial, side * per_dev, per_dev, 0)
    theirs = lax.dynamic_slice_in_dim(partial, (1 - side) * per_dev, per_dev, 0)
    theirs = lax.ppermute(theirs, "ch", [(j, j ^ 1) for j in range(n_ch)])
    spectra = mine + theirs

    whitened = whiten(spectra, F, SMOOTH)
    valid_flags = window_valid.astype(jnp.bfloat16)
    group_index = lax.axis_index("grp")
    own_flags = lax.dynamic_slice_in_dim(valid_flags, group_index, 1, 0)
    whitened = whitened * own_flags[0][:, None]
    blocks_up = (KH + per_dev - 1) // per_dev
    white_parts = [whitened]
    flag_parts = [valid_flags]
    for neighbour in range(1, blocks_up + 1):
        moved_white, moved_flags = from_behind((whitened, valid_flags), "ch", -neighbour)
        white_parts.append(moved_white)
        flag_parts.append(moved_flags)
    extended = jnp.concatenate(white_parts, axis=0)
    ext_flags = jnp.concatenate(flag_parts, axis=1)

    windows = [extended]
    for shift in range(1, n_grp):
        pairs = [(g, (g - shift) % n_grp) for g in range(n_grp)]
        windows.append(lax.ppermute(extended, "grp", pairs))
    windows = jnp.stack(windows)

    pair_full = jnp.einsum("na,nb->ab", valid_flags, ext_flags, preferred_element_type=jnp.float32)
    pair_counts = diagonal_band(pair_full, KH)
    turned = unturned(windows[:, :per_dev], -(LAGS // 2), LAGS, LAG_STEP, NT, F)
    block = jnp.einsum("walj,wbj->alb", turned, windows, preferred_element_type=jnp.float32)
    lagged = lag_band(block, KH)
    return normalise(lagged, pair_counts, band_first, band_end, F)


def solution(mesh):
    placed = (P("grp", "ch", None), P(None, "ch"), P("ch"), P("ch"))
    return jax.shard_map(
        local, mesh=mesh, in_specs=placed, out_specs=P("ch", None, None), check_vma=False
    )
```

```python
import jax
import jax.numpy as jnp
from jax import lax
from jax.experimental import pallas as pl
from jax.experimental.pallas import tpu as pltpu
from jax.sharding import PartitionSpec as P


NT = 7680
F = 384
KH = 128
SMOOTH = 65
LAGS = 32
LAG_STEP = 10


eps_white = 1e-06


def from_behind(array, axis, by):
    count = lax.axis_size(axis)
    pairs = [(i, i + by) for i in range(count) if 0 <= i + by < count]
    return lax.ppermute(array, axis, pairs)


def smoothing_matrix(bin_count, window_bins):
    row_index = jnp.arange(bin_count, dtype=jnp.int32)[:, None]
    col_index = jnp.arange(bin_count, dtype=jnp.int32)[None, :]
    distance = (row_index - col_index) % bin_count
    halfwidth = window_bins // 2
    inside = (distance <= halfwidth) | (distance >= bin_count - halfwidth)
    return inside.astype(jnp.float32)


def whiten(spectra, bin_count, window_bins):
    real_part = spectra[..., :bin_count]
    imag_part = spectra[..., bin_count:]
    magnitude = jnp.sqrt(real_part * real_part + imag_part * imag_part)
    averaged = (
        jnp.dot(
            magnitude,
            smoothing_matrix(bin_count, window_bins),
            precision=lax.Precision.HIGHEST,
            preferred_element_type=jnp.float32,
        )
        / window_bins
    )
    factor = 1.0 / (averaged + eps_white)
    return (spectra * jnp.concatenate([factor, factor], axis=-1)).astype(jnp.bfloat16)


def phase_of(index, samples):
    return (index % samples).astype(jnp.float32) * (2.0 * jnp.pi / samples)


def dft_rows(block_starts, offsets, samples, bin_count):
    orders = jnp.arange(1, bin_count + 1, dtype=jnp.int32)[None, :]
    outer = phase_of(block_starts[:, None] * orders, samples)
    inner = phase_of(offsets[:, None] * orders, samples)
    outer_cos, outer_sin = jnp.cos(outer)[:, None, :], jnp.sin(outer)[:, None, :]
    inner_cos, inner_sin = jnp.cos(inner)[None, :, :], jnp.sin(inner)[None, :, :]
    cosine = outer_cos * inner_cos - outer_sin * inner_sin
    sine_part = outer_sin * inner_cos + outer_cos * inner_sin
    table = jnp.concatenate([cosine, -sine_part], axis=-1)
    return table.reshape(-1, 2 * bin_count).astype(jnp.bfloat16)


def unturned(own, lag_first, lag_count, lag_step, samples, bin_count):
    orders = jnp.arange(1, bin_count + 1, dtype=jnp.int32)[None, :]
    shifts = ((lag_first + jnp.arange(lag_count, dtype=jnp.int32)) * lag_step)[:, None]
    phases = (shifts * orders % samples).astype(jnp.float32) * (2.0 * jnp.pi / samples)
    cosine = jnp.cos(phases)
    sine_part = jnp.sin(phases)
    real_part = own[..., :bin_count].astype(jnp.float32)[..., None, :]
    imag_part = own[..., bin_count:].astype(jnp.float32)[..., None, :]
    back_real = real_part * cosine - imag_part * sine_part
    back_imag = imag_part * cosine + real_part * sine_part
    return jnp.concatenate([back_real, back_imag], axis=-1).astype(jnp.bfloat16)


def diagonal_band(matrix, offsets):
    row_count, col_count = matrix.shape
    flat_rows = matrix.reshape(row_count * col_count)
    padded = jnp.concatenate([flat_rows, jnp.zeros((row_count,), matrix.dtype)])
    skewed = padded.reshape(row_count, col_count + 1)
    return skewed[:, :offsets]


def band_weights(pair_counts, band_lows, band_highs, bin_count):
    offsets = jnp.arange(pair_counts.shape[1], dtype=jnp.int32)[None, :]
    in_band = (offsets >= band_lows[:, None]) & (offsets < band_highs[:, None])
    return jnp.where(
        in_band, 1.0 / jnp.sqrt(float(bin_count) * jnp.maximum(pair_counts, 1.0)), 0.0
    )


def band_kernel(block_ref, weight_ref, out_ref):
    width = out_ref.shape[2]
    for row in range(out_ref.shape[0]):
        lagged = block_ref[row][:, row : row + width]
        out_ref[row] = lagged * weight_ref[row : row + 1, :]


def band_of(block, weights):
    rows, lags, _ = block.shape
    width = weights.shape[1]
    return pl.pallas_call(
        band_kernel,
        out_shape=jax.ShapeDtypeStruct((rows, lags, width), jnp.float32),
        in_specs=[pl.BlockSpec(memory_space=pltpu.VMEM)] * 2,
        out_specs=pl.BlockSpec(memory_space=pltpu.VMEM),
    )(block, weights)


def local(raw_strain, window_valid, band_first, band_end):
    n_ch = lax.axis_size("ch")
    n_grp = lax.axis_size("grp")
    _, t_here, channels = raw_strain.shape
    per_dev = channels // n_ch
    pair_width = 2 * per_dev
    half = ((t_here + 1) // 2 + 15) // 16 * 16
    me = lax.axis_index("ch")
    side = me % 2

    samples = jnp.pad(raw_strain[0], ((0, 2 * half - t_here), (0, 0)))
    samples = samples.reshape(2, half, n_ch // 2, pair_width).transpose(2, 0, 1, 3)
    samples = samples.reshape(n_ch, half, pair_width)
    samples = lax.all_to_all(samples, "ch", 0, 0, tiled=True)
    samples = samples.reshape(n_ch * half, pair_width)

    block_starts = jnp.arange(n_ch, dtype=jnp.int32) * t_here
    offsets = side * half + jnp.arange(half, dtype=jnp.int32)
    table = dft_rows(block_starts, offsets, NT, F)
    partial = jnp.einsum("tc,tf->cf", samples, table, preferred_element_type=jnp.float32)
    mine = lax.dynamic_slice_in_dim(partial, side * per_dev, per_dev, 0)
    theirs = lax.dynamic_slice_in_dim(partial, (1 - side) * per_dev, per_dev, 0)
    theirs = lax.ppermute(theirs, "ch", [(j, j ^ 1) for j in range(n_ch)])
    spectra = mine + theirs

    whitened = whiten(spectra, F, SMOOTH)
    valid_flags = window_valid.astype(jnp.bfloat16)
    group_index = lax.axis_index("grp")
    own_flags = lax.dynamic_slice_in_dim(valid_flags, group_index, 1, 0)
    whitened = whitened * own_flags[0][:, None]
    blocks_up = (KH + per_dev - 1) // per_dev
    flag_parts = [valid_flags]
    for neighbour in range(1, blocks_up + 1):
        flag_parts.append(from_behind(valid_flags, "ch", -neighbour))
    ext_flags = jnp.concatenate(flag_parts, axis=1)

    windows = []
    for shift in range(n_grp):
        parts = []
        for neighbour in range(blocks_up + 1):
            if shift == 0 and neighbour == 0:
                parts.append(whitened)
            elif shift == 0:
                parts.append(from_behind(whitened, "ch", -neighbour))
            else:
                pairs = [
                    (g * n_ch + i, ((g - shift) % n_grp) * n_ch + i - neighbour)
                    for g in range(n_grp)
                    for i in range(neighbour, n_ch)
                ]
                parts.append(lax.ppermute(whitened, ("grp", "ch"), pairs))
        windows.append(jnp.concatenate(parts, axis=0))
    windows = jnp.stack(windows)

    pair_full = jnp.einsum("na,nb->ab", valid_flags, ext_flags, preferred_element_type=jnp.float32)
    pair_counts = diagonal_band(pair_full, KH)
    turned = unturned(windows[:, :per_dev], -(LAGS // 2), LAGS, LAG_STEP, NT, F)
    block = jnp.einsum("walj,wbj->alb", turned, windows, preferred_element_type=jnp.float32)
    weights = band_weights(pair_counts, band_first, band_end, F)
    return band_of(block, weights)


def solution(mesh):
    placed = (P("grp", "ch", None), P(None, "ch"), P("ch"), P("ch"))
    return jax.shard_map(
        local, mesh=mesh, in_specs=placed, out_specs=P("ch", None, None), check_vma=False
    )
```

```python
import jax
import jax.numpy as jnp
from jax import lax
from jax.experimental import pallas as pl
from jax.experimental.pallas import tpu as pltpu
from jax.sharding import PartitionSpec as P


NT = 7680
F = 384
KH = 128
SMOOTH = 65
LAGS = 32
LAG_STEP = 10


eps_white = 1e-06


def from_behind(array, axis, by):
    count = lax.axis_size(axis)
    pairs = [(i, i + by) for i in range(count) if 0 <= i + by < count]
    return lax.ppermute(array, axis, pairs)


def smoothing_matrix(bin_count, window_bins):
    row_index = jnp.arange(bin_count, dtype=jnp.int32)[:, None]
    col_index = jnp.arange(bin_count, dtype=jnp.int32)[None, :]
    distance = (row_index - col_index) % bin_count
    halfwidth = window_bins // 2
    inside = (distance <= halfwidth) | (distance >= bin_count - halfwidth)
    return inside.astype(jnp.float32)


def whiten(spectra, bin_count, window_bins):
    real_part = spectra[..., :bin_count]
    imag_part = spectra[..., bin_count:]
    magnitude = jnp.sqrt(real_part * real_part + imag_part * imag_part)
    averaged = (
        jnp.dot(
            magnitude,
            smoothing_matrix(bin_count, window_bins),
            precision=lax.Precision.HIGHEST,
            preferred_element_type=jnp.float32,
        )
        / window_bins
    )
    factor = 1.0 / (averaged + eps_white)
    return (spectra * jnp.concatenate([factor, factor], axis=-1)).astype(jnp.bfloat16)


def phase_of(index, samples):
    return (index % samples).astype(jnp.float32) * (2.0 * jnp.pi / samples)


def dft_rows(block_starts, offsets, samples, bin_count):
    orders = jnp.arange(1, bin_count + 1, dtype=jnp.int32)[None, :]
    outer = phase_of(block_starts[:, None] * orders, samples)
    inner = phase_of(offsets[:, None] * orders, samples)
    outer_cos, outer_sin = jnp.cos(outer)[:, None, :], jnp.sin(outer)[:, None, :]
    inner_cos, inner_sin = jnp.cos(inner)[None, :, :], jnp.sin(inner)[None, :, :]
    cosine = outer_cos * inner_cos - outer_sin * inner_sin
    sine_part = outer_sin * inner_cos + outer_cos * inner_sin
    table = jnp.concatenate([cosine, -sine_part], axis=-1)
    return table.reshape(-1, 2 * bin_count).astype(jnp.bfloat16)


def unturned(own, lag_first, lag_count, lag_step, samples, bin_count):
    orders = jnp.arange(1, bin_count + 1, dtype=jnp.int32)[None, :]
    shifts = ((lag_first + jnp.arange(lag_count, dtype=jnp.int32)) * lag_step)[:, None]
    phases = (shifts * orders % samples).astype(jnp.float32) * (2.0 * jnp.pi / samples)
    cosine = jnp.cos(phases)
    sine_part = jnp.sin(phases)
    real_part = own[..., :bin_count].astype(jnp.float32)[..., None, :]
    imag_part = own[..., bin_count:].astype(jnp.float32)[..., None, :]
    back_real = real_part * cosine - imag_part * sine_part
    back_imag = imag_part * cosine + real_part * sine_part
    return jnp.concatenate([back_real, back_imag], axis=-1).astype(jnp.bfloat16)


def diagonal_band(matrix, offsets):
    row_count, col_count = matrix.shape
    flat_rows = matrix.reshape(row_count * col_count)
    padded = jnp.concatenate([flat_rows, jnp.zeros((row_count,), matrix.dtype)])
    skewed = padded.reshape(row_count, col_count + 1)
    return skewed[:, :offsets]


def band_weights(pair_counts, band_lows, band_highs, bin_count):
    offsets = jnp.arange(pair_counts.shape[1], dtype=jnp.int32)[None, :]
    in_band = (offsets >= band_lows[:, None]) & (offsets < band_highs[:, None])
    return jnp.where(
        in_band, 1.0 / jnp.sqrt(float(bin_count) * jnp.maximum(pair_counts, 1.0)), 0.0
    )


def band_kernel(block_ref, weight_ref, out_ref):
    width = out_ref.shape[2]
    lanes = block_ref.shape[2]
    for row in range(out_ref.shape[0]):
        lagged = pltpu.roll(block_ref[row], (lanes - row) % lanes, 1)[:, :width]
        out_ref[row] = lagged * weight_ref[row : row + 1, :]


def band_of(block, weights):
    rows, lags, _ = block.shape
    width = weights.shape[1]
    return pl.pallas_call(
        band_kernel,
        out_shape=jax.ShapeDtypeStruct((rows, lags, width), jnp.float32),
        in_specs=[pl.BlockSpec(memory_space=pltpu.VMEM)] * 2,
        out_specs=pl.BlockSpec(memory_space=pltpu.VMEM),
    )(block, weights)


def local(raw_strain, window_valid, band_first, band_end):
    n_ch = lax.axis_size("ch")
    n_grp = lax.axis_size("grp")
    _, t_here, channels = raw_strain.shape
    per_dev = channels // n_ch
    pair_width = 2 * per_dev
    half = ((t_here + 1) // 2 + 15) // 16 * 16
    me = lax.axis_index("ch")
    side = me % 2

    samples = jnp.pad(raw_strain[0], ((0, 2 * half - t_here), (0, 0)))
    samples = samples.reshape(2, half, n_ch // 2, pair_width).transpose(2, 0, 1, 3)
    samples = samples.reshape(n_ch, half, pair_width)
    samples = lax.all_to_all(samples, "ch", 0, 0, tiled=True)
    samples = samples.reshape(n_ch * half, pair_width)

    block_starts = jnp.arange(n_ch, dtype=jnp.int32) * t_here
    offsets = side * half + jnp.arange(half, dtype=jnp.int32)
    table = dft_rows(block_starts, offsets, NT, F)
    partial = jnp.einsum("tc,tf->cf", samples, table, preferred_element_type=jnp.float32)
    mine = lax.dynamic_slice_in_dim(partial, side * per_dev, per_dev, 0)
    theirs = lax.dynamic_slice_in_dim(partial, (1 - side) * per_dev, per_dev, 0)
    theirs = lax.ppermute(theirs, "ch", [(j, j ^ 1) for j in range(n_ch)])
    spectra = mine + theirs

    whitened = whiten(spectra, F, SMOOTH)
    valid_flags = window_valid.astype(jnp.bfloat16)
    group_index = lax.axis_index("grp")
    own_flags = lax.dynamic_slice_in_dim(valid_flags, group_index, 1, 0)
    whitened = whitened * own_flags[0][:, None]
    blocks_up = (KH + per_dev - 1) // per_dev
    white_parts = [whitened]
    flag_parts = [valid_flags]
    for neighbour in range(1, blocks_up + 1):
        moved_white, moved_flags = from_behind((whitened, valid_flags), "ch", -neighbour)
        white_parts.append(moved_white)
        flag_parts.append(moved_flags)
    extended = jnp.concatenate(white_parts, axis=0)
    ext_flags = jnp.concatenate(flag_parts, axis=1)

    windows = jnp.broadcast_to(extended[None], (n_grp,) + extended.shape)
    windows = lax.all_to_all(windows, "grp", 0, 0, tiled=True)
    lanes = 128 * pl.cdiv(extended.shape[0], 128)
    windows = jnp.pad(windows, ((0, 0), (0, lanes - extended.shape[0]), (0, 0)))

    pair_full = jnp.einsum("na,nb->ab", valid_flags, ext_flags, preferred_element_type=jnp.float32)
    pair_counts = diagonal_band(pair_full, KH)
    turned = unturned(windows[:, :per_dev], -(LAGS // 2), LAGS, LAG_STEP, NT, F)
    block = jnp.einsum("walj,wbj->alb", turned, windows, preferred_element_type=jnp.float32)
    weights = band_weights(pair_counts, band_first, band_end, F)
    return band_of(block, weights)


def solution(mesh):
    placed = (P("grp", "ch", None), P(None, "ch"), P("ch"), P("ch"))
    return jax.shard_map(
        local, mesh=mesh, in_specs=placed, out_specs=P("ch", None, None), check_vma=False
    )
```

```python
import jax
import jax.numpy as jnp
from jax import lax
from jax.experimental import pallas as pl
from jax.experimental.pallas import tpu as pltpu
from jax.sharding import PartitionSpec as P


NT = 7680
F = 384
KH = 128
SMOOTH = 65
LAGS = 32
LAG_STEP = 10


eps_white = 1e-06


def from_behind(array, axis, by):
    count = lax.axis_size(axis)
    pairs = [(i, i + by) for i in range(count) if 0 <= i + by < count]
    return lax.ppermute(array, axis, pairs)


def smoothing_matrix(bin_count, window_bins):
    row_index = jnp.arange(bin_count, dtype=jnp.int32)[:, None]
    col_index = jnp.arange(bin_count, dtype=jnp.int32)[None, :]
    distance = (row_index - col_index) % bin_count
    halfwidth = window_bins // 2
    inside = (distance <= halfwidth) | (distance >= bin_count - halfwidth)
    return inside.astype(jnp.float32)


def whiten(spectra, bin_count, window_bins):
    real_part = spectra[..., :bin_count]
    imag_part = spectra[..., bin_count:]
    magnitude = jnp.sqrt(real_part * real_part + imag_part * imag_part)
    averaged = (
        jnp.dot(
            magnitude,
            smoothing_matrix(bin_count, window_bins),
            precision=lax.Precision.HIGHEST,
            preferred_element_type=jnp.float32,
        )
        / window_bins
    )
    factor = 1.0 / (averaged + eps_white)
    return (spectra * jnp.concatenate([factor, factor], axis=-1)).astype(jnp.bfloat16)


def phase_of(index, samples):
    return (index % samples).astype(jnp.float32) * (2.0 * jnp.pi / samples)


def dft_rows(block_starts, offsets, samples, bin_count):
    orders = jnp.arange(1, bin_count + 1, dtype=jnp.int32)[None, :]
    outer = phase_of(block_starts[:, None] * orders, samples)
    inner = phase_of(offsets[:, None] * orders, samples)
    outer_cos, outer_sin = jnp.cos(outer)[:, None, :], jnp.sin(outer)[:, None, :]
    inner_cos, inner_sin = jnp.cos(inner)[None, :, :], jnp.sin(inner)[None, :, :]
    cosine = outer_cos * inner_cos - outer_sin * inner_sin
    sine_part = outer_sin * inner_cos + outer_cos * inner_sin
    table = jnp.concatenate([cosine, -sine_part], axis=-1)
    return table.reshape(-1, 2 * bin_count).astype(jnp.bfloat16)


def unturned(own, lag_first, lag_count, lag_step, samples, bin_count):
    orders = jnp.arange(1, bin_count + 1, dtype=jnp.int32)[None, :]
    shifts = ((lag_first + jnp.arange(lag_count, dtype=jnp.int32)) * lag_step)[:, None]
    phases = (shifts * orders % samples).astype(jnp.float32) * (2.0 * jnp.pi / samples)
    cosine = jnp.cos(phases)
    sine_part = jnp.sin(phases)
    real_part = own[..., :bin_count].astype(jnp.float32)[..., None, :]
    imag_part = own[..., bin_count:].astype(jnp.float32)[..., None, :]
    back_real = real_part * cosine - imag_part * sine_part
    back_imag = imag_part * cosine + real_part * sine_part
    return jnp.concatenate([back_real, back_imag], axis=-1).astype(jnp.bfloat16)


def diagonal_band(matrix, offsets):
    row_count, col_count = matrix.shape
    flat_rows = matrix.reshape(row_count * col_count)
    padded = jnp.concatenate([flat_rows, jnp.zeros((row_count,), matrix.dtype)])
    skewed = padded.reshape(row_count, col_count + 1)
    return skewed[:, :offsets]


def band_weights(pair_counts, band_lows, band_highs, bin_count):
    offsets = jnp.arange(pair_counts.shape[1], dtype=jnp.int32)[None, :]
    in_band = (offsets >= band_lows[:, None]) & (offsets < band_highs[:, None])
    return jnp.where(
        in_band, 1.0 / jnp.sqrt(float(bin_count) * jnp.maximum(pair_counts, 1.0)), 0.0
    )


def band_kernel(block_ref, weight_ref, out_ref):
    width = out_ref.shape[2]
    lanes = block_ref.shape[2]
    for row in range(out_ref.shape[0]):
        lagged = pltpu.roll(block_ref[row], (lanes - row) % lanes, 1)[:, :width]
        out_ref[row] = lagged * weight_ref[row : row + 1, :]


def band_of(block, weights):
    rows, lags, _ = block.shape
    width = weights.shape[1]
    return pl.pallas_call(
        band_kernel,
        out_shape=jax.ShapeDtypeStruct((rows, lags, width), jnp.float32),
        in_specs=[pl.BlockSpec(memory_space=pltpu.VMEM)] * 2,
        out_specs=pl.BlockSpec(memory_space=pltpu.VMEM),
    )(block, weights)


def local(raw_strain, window_valid, band_first, band_end):
    n_ch = lax.axis_size("ch")
    n_grp = lax.axis_size("grp")
    _, t_here, channels = raw_strain.shape
    per_dev = channels // n_ch
    pair_width = 2 * per_dev
    half = ((t_here + 1) // 2 + 15) // 16 * 16
    me = lax.axis_index("ch")
    side = me % 2

    samples = jnp.pad(raw_strain[0], ((0, 2 * half - t_here), (0, 0)))
    samples = samples.reshape(2, half, n_ch // 2, pair_width).transpose(2, 0, 1, 3)
    samples = samples.reshape(n_ch, half, pair_width)
    samples = lax.all_to_all(samples, "ch", 0, 0, tiled=True)
    samples = samples.reshape(n_ch * half, pair_width)

    block_starts = jnp.arange(n_ch, dtype=jnp.int32) * t_here
    offsets = side * half + jnp.arange(half, dtype=jnp.int32)
    table = dft_rows(block_starts, offsets, NT, F)
    partial = jnp.einsum("tc,tf->cf", samples, table, preferred_element_type=jnp.float32)
    mine = lax.dynamic_slice_in_dim(partial, side * per_dev, per_dev, 0)
    theirs = lax.dynamic_slice_in_dim(partial, (1 - side) * per_dev, per_dev, 0)
    theirs = lax.ppermute(theirs, "ch", [(j, j ^ 1) for j in range(n_ch)])
    spectra = mine + theirs

    whitened = whiten(spectra, F, SMOOTH)
    valid_flags = window_valid.astype(jnp.bfloat16)
    group_index = lax.axis_index("grp")
    own_flags = lax.dynamic_slice_in_dim(valid_flags, group_index, 1, 0)
    whitened = whitened * own_flags[0][:, None]
    blocks_up = (KH + per_dev - 1) // per_dev
    own_rows = jnp.broadcast_to(whitened[None], (n_grp,) + whitened.shape)
    own_rows = lax.all_to_all(own_rows, "grp", 0, 0, tiled=True)
    white_parts = [own_rows]
    flag_parts = [valid_flags]
    for neighbour in range(1, blocks_up + 1):
        moved_white, moved_flags = from_behind((own_rows, valid_flags), "ch", -neighbour)
        white_parts.append(moved_white)
        flag_parts.append(moved_flags)
    rows_used = per_dev * (blocks_up + 1)
    lanes = 128 * pl.cdiv(rows_used, 128)
    white_parts.append(jnp.zeros((n_grp, lanes - rows_used, 2 * F), jnp.bfloat16))
    windows = jnp.concatenate(white_parts, axis=1)
    ext_flags = jnp.concatenate(flag_parts, axis=1)

    pair_full = jnp.einsum("na,nb->ab", valid_flags, ext_flags, preferred_element_type=jnp.float32)
    pair_counts = diagonal_band(pair_full, KH)
    turned = unturned(own_rows, -(LAGS // 2), LAGS, LAG_STEP, NT, F)
    block = jnp.einsum("walj,wbj->alb", turned, windows, preferred_element_type=jnp.float32)
    weights = band_weights(pair_counts, band_first, band_end, F)
    return band_of(block, weights)


def solution(mesh):
    placed = (P("grp", "ch", None), P(None, "ch"), P("ch"), P("ch"))
    return jax.shard_map(
        local, mesh=mesh, in_specs=placed, out_specs=P("ch", None, None), check_vma=False
    )
```

```python
import jax
import jax.numpy as jnp
from jax import lax
from jax.experimental import pallas as pl
from jax.experimental.pallas import tpu as pltpu
from jax.sharding import PartitionSpec as P


NT = 7680
F = 384
KH = 128
SMOOTH = 65
LAGS = 32
LAG_STEP = 10


eps_white = 1e-06


def from_behind(array, axis, by):
    count = lax.axis_size(axis)
    pairs = [(i, i + by) for i in range(count) if 0 <= i + by < count]
    return lax.ppermute(array, axis, pairs)


def smoothing_matrix(bin_count, window_bins):
    row_index = jnp.arange(bin_count, dtype=jnp.int32)[:, None]
    col_index = jnp.arange(bin_count, dtype=jnp.int32)[None, :]
    distance = (row_index - col_index) % bin_count
    halfwidth = window_bins // 2
    inside = (distance <= halfwidth) | (distance >= bin_count - halfwidth)
    return inside.astype(jnp.float32)


def whiten(spectra, bin_count, window_bins):
    real_part = spectra[..., :bin_count]
    imag_part = spectra[..., bin_count:]
    magnitude = jnp.sqrt(real_part * real_part + imag_part * imag_part)
    averaged = (
        jnp.dot(
            magnitude,
            smoothing_matrix(bin_count, window_bins),
            precision=lax.Precision.HIGHEST,
            preferred_element_type=jnp.float32,
        )
        / window_bins
    )
    factor = 1.0 / (averaged + eps_white)
    return (spectra * jnp.concatenate([factor, factor], axis=-1)).astype(jnp.bfloat16)


def phase_of(index, samples):
    return (index % samples).astype(jnp.float32) * (2.0 * jnp.pi / samples)


def dft_rows(block_starts, offsets, samples, bin_count):
    orders = jnp.arange(1, bin_count + 1, dtype=jnp.int32)[None, :]
    outer = phase_of(block_starts[:, None] * orders, samples)
    inner = phase_of(offsets[:, None] * orders, samples)
    outer_cos, outer_sin = jnp.cos(outer)[:, None, :], jnp.sin(outer)[:, None, :]
    inner_cos, inner_sin = jnp.cos(inner)[None, :, :], jnp.sin(inner)[None, :, :]
    cosine = outer_cos * inner_cos - outer_sin * inner_sin
    sine_part = outer_sin * inner_cos + outer_cos * inner_sin
    table = jnp.concatenate([cosine, -sine_part], axis=-1)
    return table.reshape(-1, 2 * bin_count).astype(jnp.bfloat16)


def unturned(own, lag_first, lag_count, lag_step, samples, bin_count):
    orders = jnp.arange(1, bin_count + 1, dtype=jnp.int32)[None, :]
    shifts = ((lag_first + jnp.arange(lag_count, dtype=jnp.int32)) * lag_step)[:, None]
    phases = (shifts * orders % samples).astype(jnp.float32) * (2.0 * jnp.pi / samples)
    cosine = jnp.cos(phases)
    sine_part = jnp.sin(phases)
    real_part = own[..., :bin_count].astype(jnp.float32)[..., None, :]
    imag_part = own[..., bin_count:].astype(jnp.float32)[..., None, :]
    back_real = real_part * cosine - imag_part * sine_part
    back_imag = imag_part * cosine + real_part * sine_part
    return jnp.concatenate([back_real, back_imag], axis=-1).astype(jnp.bfloat16)


def diagonal_band(matrix, offsets):
    row_count, col_count = matrix.shape
    flat_rows = matrix.reshape(row_count * col_count)
    padded = jnp.concatenate([flat_rows, jnp.zeros((row_count,), matrix.dtype)])
    skewed = padded.reshape(row_count, col_count + 1)
    return skewed[:, :offsets]


def band_weights(pair_counts, band_lows, band_highs, bin_count):
    offsets = jnp.arange(pair_counts.shape[1], dtype=jnp.int32)[None, :]
    in_band = (offsets >= band_lows[:, None]) & (offsets < band_highs[:, None])
    return jnp.where(
        in_band, 1.0 / jnp.sqrt(float(bin_count) * jnp.maximum(pair_counts, 1.0)), 0.0
    )


def corr_kernel(turned_ref, windows_ref, weight_ref, out_ref):
    n_win, rows, lags, depth = turned_ref.shape
    lanes = windows_ref.shape[1]
    width = out_ref.shape[2]
    first = pl.program_id(0) * rows
    total = jnp.zeros((rows * lags, lanes), jnp.float32)
    for window in range(n_win):
        lhs = turned_ref[window].reshape(rows * lags, depth)
        total += lax.dot_general(
            lhs, windows_ref[window], (((1,), (1,)), ((), ())), preferred_element_type=jnp.float32
        )
    for row in range(rows):
        shift = (lanes - first - row) % lanes
        lagged = pltpu.roll(total[row * lags : (row + 1) * lags], shift, 1)[:, :width]
        out_ref[row] = lagged * weight_ref[row : row + 1, :]


def correlate(turned, windows, weights, rows=8):
    n_win, own, lags, depth = turned.shape
    lanes = windows.shape[1]
    width = weights.shape[1]
    return pl.pallas_call(
        corr_kernel,
        out_shape=jax.ShapeDtypeStruct((own, lags, width), jnp.float32),
        grid=(own // rows,),
        in_specs=[
            pl.BlockSpec((n_win, rows, lags, depth), lambda i: (0, i, 0, 0)),
            pl.BlockSpec((n_win, lanes, depth), lambda i: (0, 0, 0)),
            pl.BlockSpec((rows, width), lambda i: (i, 0)),
        ],
        out_specs=pl.BlockSpec((rows, lags, width), lambda i: (i, 0, 0)),
        cost_estimate=pl.CostEstimate(
            flops=2 * n_win * own * lags * depth * lanes,
            bytes_accessed=2 * turned.size + 2 * windows.size + 4 * own * lags * width,
            transcendentals=0,
        ),
    )(turned, windows, weights)


def local(raw_strain, window_valid, band_first, band_end):
    n_ch = lax.axis_size("ch")
    n_grp = lax.axis_size("grp")
    _, t_here, channels = raw_strain.shape
    per_dev = channels // n_ch
    pair_width = 2 * per_dev
    half = ((t_here + 1) // 2 + 15) // 16 * 16
    me = lax.axis_index("ch")
    side = me % 2

    samples = jnp.pad(raw_strain[0], ((0, 2 * half - t_here), (0, 0)))
    samples = samples.reshape(2, half, n_ch // 2, pair_width).transpose(2, 0, 1, 3)
    samples = samples.reshape(n_ch, half, pair_width)
    samples = lax.all_to_all(samples, "ch", 0, 0, tiled=True)
    samples = samples.reshape(n_ch * half, pair_width)

    block_starts = jnp.arange(n_ch, dtype=jnp.int32) * t_here
    offsets = side * half + jnp.arange(half, dtype=jnp.int32)
    table = dft_rows(block_starts, offsets, NT, F)
    partial = jnp.einsum("tc,tf->cf", samples, table, preferred_element_type=jnp.float32)
    mine = lax.dynamic_slice_in_dim(partial, side * per_dev, per_dev, 0)
    theirs = lax.dynamic_slice_in_dim(partial, (1 - side) * per_dev, per_dev, 0)
    theirs = lax.ppermute(theirs, "ch", [(j, j ^ 1) for j in range(n_ch)])
    spectra = mine + theirs

    whitened = whiten(spectra, F, SMOOTH)
    valid_flags = window_valid.astype(jnp.bfloat16)
    group_index = lax.axis_index("grp")
    own_flags = lax.dynamic_slice_in_dim(valid_flags, group_index, 1, 0)
    whitened = whitened * own_flags[0][:, None]
    blocks_up = (KH + per_dev - 1) // per_dev
    own_rows = jnp.broadcast_to(whitened[None], (n_grp,) + whitened.shape)
    own_rows = lax.all_to_all(own_rows, "grp", 0, 0, tiled=True)
    white_parts = [own_rows]
    flag_parts = [valid_flags]
    for neighbour in range(1, blocks_up + 1):
        moved_white, moved_flags = from_behind((own_rows, valid_flags), "ch", -neighbour)
        white_parts.append(moved_white)
        flag_parts.append(moved_flags)
    rows_used = per_dev * (blocks_up + 1)
    lanes = 128 * pl.cdiv(rows_used, 128)
    white_parts.append(jnp.zeros((n_grp, lanes - rows_used, 2 * F), jnp.bfloat16))
    windows = jnp.concatenate(white_parts, axis=1)
    ext_flags = jnp.concatenate(flag_parts, axis=1)

    pair_full = jnp.einsum("na,nb->ab", valid_flags, ext_flags, preferred_element_type=jnp.float32)
    pair_counts = diagonal_band(pair_full, KH)
    turned = unturned(own_rows, -(LAGS // 2), LAGS, LAG_STEP, NT, F)
    weights = band_weights(pair_counts, band_first, band_end, F)
    return correlate(turned, windows, weights)


def solution(mesh):
    placed = (P("grp", "ch", None), P(None, "ch"), P("ch"), P("ch"))
    return jax.shard_map(
        local, mesh=mesh, in_specs=placed, out_specs=P("ch", None, None), check_vma=False
    )
```

```python
import jax
import jax.numpy as jnp
from jax import lax
from jax.experimental import pallas as pl
from jax.experimental.pallas import tpu as pltpu
from jax.sharding import PartitionSpec as P


NT = 7680
F = 384
KH = 128
SMOOTH = 65
LAGS = 32
LAG_STEP = 10


eps_white = 1e-06


def from_behind(array, axis, by):
    count = lax.axis_size(axis)
    pairs = [(i, i + by) for i in range(count) if 0 <= i + by < count]
    return lax.ppermute(array, axis, pairs)


def smoothing_matrix(bin_count, window_bins):
    row_index = jnp.arange(bin_count, dtype=jnp.int32)[:, None]
    col_index = jnp.arange(bin_count, dtype=jnp.int32)[None, :]
    distance = (row_index - col_index) % bin_count
    halfwidth = window_bins // 2
    inside = (distance <= halfwidth) | (distance >= bin_count - halfwidth)
    return inside.astype(jnp.float32)


def whiten(spectra, bin_count, window_bins):
    real_part = spectra[..., :bin_count]
    imag_part = spectra[..., bin_count:]
    magnitude = jnp.sqrt(real_part * real_part + imag_part * imag_part)
    averaged = (
        jnp.dot(
            magnitude,
            smoothing_matrix(bin_count, window_bins),
            precision=lax.Precision.HIGHEST,
            preferred_element_type=jnp.float32,
        )
        / window_bins
    )
    factor = 1.0 / (averaged + eps_white)
    return (spectra * jnp.concatenate([factor, factor], axis=-1)).astype(jnp.bfloat16)


def phase_of(index, samples):
    return (index % samples).astype(jnp.float32) * (2.0 * jnp.pi / samples)


def dft_rows(block_starts, offsets, samples, bin_count):
    orders = jnp.arange(1, bin_count + 1, dtype=jnp.int32)[None, :]
    outer = phase_of(block_starts[:, None] * orders, samples)
    inner = phase_of(offsets[:, None] * orders, samples)
    outer_cos, outer_sin = jnp.cos(outer)[:, None, :], jnp.sin(outer)[:, None, :]
    inner_cos, inner_sin = jnp.cos(inner)[None, :, :], jnp.sin(inner)[None, :, :]
    cosine = outer_cos * inner_cos - outer_sin * inner_sin
    sine_part = outer_sin * inner_cos + outer_cos * inner_sin
    table = jnp.concatenate([cosine, -sine_part], axis=-1)
    return table.reshape(-1, 2 * bin_count).astype(jnp.bfloat16)


def unturned(own, lag_first, lag_count, lag_step, samples, bin_count):
    orders = jnp.arange(1, bin_count + 1, dtype=jnp.int32)[None, :]
    shifts = ((lag_first + jnp.arange(lag_count, dtype=jnp.int32)) * lag_step)[:, None]
    phases = (shifts * orders % samples).astype(jnp.float32) * (2.0 * jnp.pi / samples)
    cosine = jnp.cos(phases)
    sine_part = jnp.sin(phases)
    real_part = own[..., :bin_count].astype(jnp.float32)[..., None, :]
    imag_part = own[..., bin_count:].astype(jnp.float32)[..., None, :]
    back_real = real_part * cosine - imag_part * sine_part
    back_imag = imag_part * cosine + real_part * sine_part
    return jnp.concatenate([back_real, back_imag], axis=-1).astype(jnp.bfloat16)


def diagonal_band(matrix, offsets):
    row_count, col_count = matrix.shape
    flat_rows = matrix.reshape(row_count * col_count)
    padded = jnp.concatenate([flat_rows, jnp.zeros((row_count,), matrix.dtype)])
    skewed = padded.reshape(row_count, col_count + 1)
    return skewed[:, :offsets]


def band_weights(pair_counts, band_lows, band_highs, bin_count):
    offsets = jnp.arange(pair_counts.shape[1], dtype=jnp.int32)[None, :]
    in_band = (offsets >= band_lows[:, None]) & (offsets < band_highs[:, None])
    return jnp.where(
        in_band, 1.0 / jnp.sqrt(float(bin_count) * jnp.maximum(pair_counts, 1.0)), 0.0
    )


def band_kernel(block_ref, weight_ref, out_ref):
    width = out_ref.shape[2]
    lanes = block_ref.shape[2]
    for row in range(out_ref.shape[0]):
        lagged = pltpu.roll(block_ref[row], (lanes - row) % lanes, 1)[:, :width]
        out_ref[row] = lagged * weight_ref[row : row + 1, :]


def band_of(block, weights):
    rows, lags, _ = block.shape
    width = weights.shape[1]
    return pl.pallas_call(
        band_kernel,
        out_shape=jax.ShapeDtypeStruct((rows, lags, width), jnp.float32),
        in_specs=[pl.BlockSpec(memory_space=pltpu.VMEM)] * 2,
        out_specs=pl.BlockSpec(memory_space=pltpu.VMEM),
    )(block, weights)


def local(raw_strain, window_valid, band_first, band_end):
    n_ch = lax.axis_size("ch")
    n_grp = lax.axis_size("grp")
    _, t_here, channels = raw_strain.shape
    per_dev = channels // n_ch
    pair_width = 2 * per_dev
    half = ((t_here + 1) // 2 + 15) // 16 * 16
    me = lax.axis_index("ch")
    side = me % 2

    samples = jnp.pad(raw_strain[0], ((0, 2 * half - t_here), (0, 0)))
    samples = samples.reshape(2, half, n_ch // 2, 2, per_dev).transpose(2, 3, 1, 0, 4)
    samples = samples.reshape(n_ch, half, 2 * per_dev)
    samples = lax.all_to_all(samples, "ch", 0, 0, tiled=True)
    samples = samples.reshape(n_ch, half, 2, per_dev)

    block_starts = jnp.arange(n_ch, dtype=jnp.int32) * t_here
    offsets = jnp.arange(2 * half, dtype=jnp.int32)
    table = dft_rows(block_starts, offsets, NT, F).reshape(n_ch, 2, half, 2 * F)
    spectra = jnp.einsum("srhc,shrf->cf", samples, table, preferred_element_type=jnp.float32)

    whitened = whiten(spectra, F, SMOOTH)
    valid_flags = window_valid.astype(jnp.bfloat16)
    group_index = lax.axis_index("grp")
    own_flags = lax.dynamic_slice_in_dim(valid_flags, group_index, 1, 0)
    whitened = whitened * own_flags[0][:, None]
    blocks_up = (KH + per_dev - 1) // per_dev
    own_rows = jnp.broadcast_to(whitened[None], (n_grp,) + whitened.shape)
    own_rows = lax.all_to_all(own_rows, "grp", 0, 0, tiled=True)
    white_parts = [own_rows]
    flag_parts = [valid_flags]
    for neighbour in range(1, blocks_up + 1):
        moved_white, moved_flags = from_behind((own_rows, valid_flags), "ch", -neighbour)
        white_parts.append(moved_white)
        flag_parts.append(moved_flags)
    rows_used = per_dev * (blocks_up + 1)
    lanes = 128 * pl.cdiv(rows_used, 128)
    white_parts.append(jnp.zeros((n_grp, lanes - rows_used, 2 * F), jnp.bfloat16))
    windows = jnp.concatenate(white_parts, axis=1)
    ext_flags = jnp.concatenate(flag_parts, axis=1)

    pair_full = jnp.einsum("na,nb->ab", valid_flags, ext_flags, preferred_element_type=jnp.float32)
    pair_counts = diagonal_band(pair_full, KH)
    turned = unturned(own_rows, -(LAGS // 2), LAGS, LAG_STEP, NT, F)
    block = jnp.einsum("walj,wbj->alb", turned, windows, preferred_element_type=jnp.float32)
    weights = band_weights(pair_counts, band_first, band_end, F)
    return band_of(block, weights)


def solution(mesh):
    placed = (P("grp", "ch", None), P(None, "ch"), P("ch"), P("ch"))
    return jax.shard_map(
        local, mesh=mesh, in_specs=placed, out_specs=P("ch", None, None), check_vma=False
    )
```

```python
import jax
import jax.numpy as jnp
from jax import lax
from jax.experimental import pallas as pl
from jax.experimental.pallas import tpu as pltpu
from jax.sharding import PartitionSpec as P


NT = 7680
F = 384
KH = 128
SMOOTH = 65
LAGS = 32
LAG_STEP = 10


eps_white = 1e-06


def from_behind(array, axis, by):
    count = lax.axis_size(axis)
    pairs = [(i, i + by) for i in range(count) if 0 <= i + by < count]
    return lax.ppermute(array, axis, pairs)


def smoothing_matrix(bin_count, window_bins):
    row_index = jnp.arange(bin_count, dtype=jnp.int32)[:, None]
    col_index = jnp.arange(bin_count, dtype=jnp.int32)[None, :]
    distance = (row_index - col_index) % bin_count
    halfwidth = window_bins // 2
    inside = (distance <= halfwidth) | (distance >= bin_count - halfwidth)
    return inside.astype(jnp.float32)


def whiten(spectra, bin_count, window_bins):
    real_part = spectra[..., :bin_count]
    imag_part = spectra[..., bin_count:]
    magnitude = jnp.sqrt(real_part * real_part + imag_part * imag_part)
    averaged = (
        jnp.dot(
            magnitude,
            smoothing_matrix(bin_count, window_bins),
            precision=lax.Precision.HIGHEST,
            preferred_element_type=jnp.float32,
        )
        / window_bins
    )
    factor = 1.0 / (averaged + eps_white)
    return (spectra * jnp.concatenate([factor, factor], axis=-1)).astype(jnp.bfloat16)


def phase_of(index, samples):
    return (index % samples).astype(jnp.float32) * (2.0 * jnp.pi / samples)


def dft_rows(block_starts, offsets, samples, bin_count):
    orders = jnp.arange(1, bin_count + 1, dtype=jnp.int32)[None, :]
    outer = phase_of(block_starts[:, None] * orders, samples)
    inner = phase_of(offsets[:, None] * orders, samples)
    outer_cos, outer_sin = jnp.cos(outer)[:, None, :], jnp.sin(outer)[:, None, :]
    inner_cos, inner_sin = jnp.cos(inner)[None, :, :], jnp.sin(inner)[None, :, :]
    cosine = outer_cos * inner_cos - outer_sin * inner_sin
    sine_part = outer_sin * inner_cos + outer_cos * inner_sin
    table = jnp.concatenate([cosine, -sine_part], axis=-1)
    return table.reshape(-1, 2 * bin_count).astype(jnp.bfloat16)


def unturned(own, lag_first, lag_count, lag_step, samples, bin_count):
    orders = jnp.arange(1, bin_count + 1, dtype=jnp.int32)[None, :]
    shifts = ((lag_first + jnp.arange(lag_count, dtype=jnp.int32)) * lag_step)[:, None]
    phases = (shifts * orders % samples).astype(jnp.float32) * (2.0 * jnp.pi / samples)
    cosine = jnp.cos(phases)
    sine_part = jnp.sin(phases)
    real_part = own[..., :bin_count].astype(jnp.float32)[..., None, :]
    imag_part = own[..., bin_count:].astype(jnp.float32)[..., None, :]
    back_real = real_part * cosine - imag_part * sine_part
    back_imag = imag_part * cosine + real_part * sine_part
    return jnp.concatenate([back_real, back_imag], axis=-1).astype(jnp.bfloat16)


def diagonal_band(matrix, offsets):
    row_count, col_count = matrix.shape
    flat_rows = matrix.reshape(row_count * col_count)
    padded = jnp.concatenate([flat_rows, jnp.zeros((row_count,), matrix.dtype)])
    skewed = padded.reshape(row_count, col_count + 1)
    return skewed[:, :offsets]


def band_weights(pair_counts, band_lows, band_highs, bin_count):
    offsets = jnp.arange(pair_counts.shape[1], dtype=jnp.int32)[None, :]
    in_band = (offsets >= band_lows[:, None]) & (offsets < band_highs[:, None])
    return jnp.where(
        in_band, 1.0 / jnp.sqrt(float(bin_count) * jnp.maximum(pair_counts, 1.0)), 0.0
    )


def band_kernel(block_ref, weight_ref, out_ref):
    width = out_ref.shape[2]
    lanes = block_ref.shape[2]
    for row in range(out_ref.shape[0]):
        lagged = pltpu.roll(block_ref[row], (lanes - row) % lanes, 1)[:, :width]
        out_ref[row] = lagged * weight_ref[row : row + 1, :]


def band_of(block, weights):
    rows, lags, _ = block.shape
    width = weights.shape[1]
    return pl.pallas_call(
        band_kernel,
        out_shape=jax.ShapeDtypeStruct((rows, lags, width), jnp.float32),
        in_specs=[pl.BlockSpec(memory_space=pltpu.VMEM)] * 2,
        out_specs=pl.BlockSpec(memory_space=pltpu.VMEM),
    )(block, weights)


def pack_kernel(raw_ref, out_ref, pad_ref):
    rows = raw_ref.shape[1]
    half, lanes = out_ref.shape[1], out_ref.shape[2]
    pad_ref[...] = jnp.zeros(pad_ref.shape, jnp.float32)
    lane = lax.broadcasted_iota(jnp.int32, (half, lanes), 1)
    low = lane < lanes // 2
    for tile in range(out_ref.shape[0] // 2):
        pad_ref[:rows] = raw_ref[0, :, tile * lanes : (tile + 1) * lanes].astype(jnp.float32)
        top, bottom = pad_ref[:half], pad_ref[half:]
        even = jnp.where(low, top, pltpu.roll(bottom, lanes // 2, 1))
        odd = jnp.where(low, pltpu.roll(top, lanes // 2, 1), bottom)
        out_ref[2 * tile] = even.astype(out_ref.dtype)
        out_ref[2 * tile + 1] = odd.astype(out_ref.dtype)


def pack(raw_strain, half, tiles_per_step=8):
    _, rows, channels = raw_strain.shape
    lanes = 128
    tiles = channels // lanes
    return pl.pallas_call(
        pack_kernel,
        out_shape=jax.ShapeDtypeStruct((2 * tiles, half, lanes), raw_strain.dtype),
        grid=(tiles // tiles_per_step,),
        in_specs=[pl.BlockSpec((1, rows, tiles_per_step * lanes), lambda i: (0, 0, i))],
        out_specs=pl.BlockSpec((2 * tiles_per_step, half, lanes), lambda i: (i, 0, 0)),
        scratch_shapes=[pltpu.VMEM((2 * half, lanes), jnp.float32)],
    )(raw_strain)


def local(raw_strain, window_valid, band_first, band_end):
    n_ch = lax.axis_size("ch")
    n_grp = lax.axis_size("grp")
    _, t_here, channels = raw_strain.shape
    per_dev = channels // n_ch
    pair_width = 2 * per_dev
    half = ((t_here + 1) // 2 + 15) // 16 * 16
    me = lax.axis_index("ch")
    side = me % 2

    samples = pack(raw_strain, half)
    samples = lax.all_to_all(samples, "ch", 0, 0, tiled=True)
    samples = samples.reshape(n_ch, half, 2, per_dev)

    block_starts = jnp.arange(n_ch, dtype=jnp.int32) * t_here
    offsets = jnp.arange(2 * half, dtype=jnp.int32)
    table = dft_rows(block_starts, offsets, NT, F).reshape(n_ch, 2, half, 2 * F)
    spectra = jnp.einsum("srhc,shrf->cf", samples, table, preferred_element_type=jnp.float32)

    whitened = whiten(spectra, F, SMOOTH)
    valid_flags = window_valid.astype(jnp.bfloat16)
    group_index = lax.axis_index("grp")
    own_flags = lax.dynamic_slice_in_dim(valid_flags, group_index, 1, 0)
    whitened = whitened * own_flags[0][:, None]
    blocks_up = (KH + per_dev - 1) // per_dev
    own_rows = jnp.broadcast_to(whitened[None], (n_grp,) + whitened.shape)
    own_rows = lax.all_to_all(own_rows, "grp", 0, 0, tiled=True)
    white_parts = [own_rows]
    flag_parts = [valid_flags]
    for neighbour in range(1, blocks_up + 1):
        moved_white, moved_flags = from_behind((own_rows, valid_flags), "ch", -neighbour)
        white_parts.append(moved_white)
        flag_parts.append(moved_flags)
    rows_used = per_dev * (blocks_up + 1)
    lanes = 128 * pl.cdiv(rows_used, 128)
    white_parts.append(jnp.zeros((n_grp, lanes - rows_used, 2 * F), jnp.bfloat16))
    windows = jnp.concatenate(white_parts, axis=1)
    ext_flags = jnp.concatenate(flag_parts, axis=1)

    pair_full = jnp.einsum("na,nb->ab", valid_flags, ext_flags, preferred_element_type=jnp.float32)
    pair_counts = diagonal_band(pair_full, KH)
    turned = unturned(own_rows, -(LAGS // 2), LAGS, LAG_STEP, NT, F)
    block = jnp.einsum("walj,wbj->alb", turned, windows, preferred_element_type=jnp.float32)
    weights = band_weights(pair_counts, band_first, band_end, F)
    return band_of(block, weights)


def solution(mesh):
    placed = (P("grp", "ch", None), P(None, "ch"), P("ch"), P("ch"))
    return jax.shard_map(
        local, mesh=mesh, in_specs=placed, out_specs=P("ch", None, None), check_vma=False
    )
```

```python
import jax
import jax.numpy as jnp
from jax import lax
from jax.experimental import pallas as pl
from jax.experimental.pallas import tpu as pltpu
from jax.sharding import PartitionSpec as P


NT = 7680
F = 384
KH = 128
SMOOTH = 65
LAGS = 32
LAG_STEP = 10


eps_white = 1e-06


def from_behind(array, axis, by):
    count = lax.axis_size(axis)
    pairs = [(i, i + by) for i in range(count) if 0 <= i + by < count]
    return lax.ppermute(array, axis, pairs)


def smoothing_matrix(bin_count, window_bins):
    row_index = jnp.arange(bin_count, dtype=jnp.int32)[:, None]
    col_index = jnp.arange(bin_count, dtype=jnp.int32)[None, :]
    distance = (row_index - col_index) % bin_count
    halfwidth = window_bins // 2
    inside = (distance <= halfwidth) | (distance >= bin_count - halfwidth)
    return inside.astype(jnp.float32)


def whiten(spectra, bin_count, window_bins):
    real_part = spectra[..., :bin_count]
    imag_part = spectra[..., bin_count:]
    magnitude = jnp.sqrt(real_part * real_part + imag_part * imag_part)
    averaged = (
        jnp.dot(
            magnitude,
            smoothing_matrix(bin_count, window_bins),
            precision=lax.Precision.HIGHEST,
            preferred_element_type=jnp.float32,
        )
        / window_bins
    )
    factor = 1.0 / (averaged + eps_white)
    return (spectra * jnp.concatenate([factor, factor], axis=-1)).astype(jnp.bfloat16)


def phase_of(index, samples):
    return (index % samples).astype(jnp.float32) * (2.0 * jnp.pi / samples)


def dft_rows(block_starts, offsets, samples, bin_count):
    orders = jnp.arange(1, bin_count + 1, dtype=jnp.int32)[None, :]
    outer = phase_of(block_starts[:, None] * orders, samples)
    inner = phase_of(offsets[:, None] * orders, samples)
    outer_cos, outer_sin = jnp.cos(outer)[:, None, :], jnp.sin(outer)[:, None, :]
    inner_cos, inner_sin = jnp.cos(inner)[None, :, :], jnp.sin(inner)[None, :, :]
    cosine = outer_cos * inner_cos - outer_sin * inner_sin
    sine_part = outer_sin * inner_cos + outer_cos * inner_sin
    table = jnp.concatenate([cosine, -sine_part], axis=-1)
    return table.reshape(-1, 2 * bin_count).astype(jnp.bfloat16)


def unturned(own, lag_first, lag_count, lag_step, samples, bin_count):
    orders = jnp.arange(1, bin_count + 1, dtype=jnp.int32)[None, :]
    shifts = ((lag_first + jnp.arange(lag_count, dtype=jnp.int32)) * lag_step)[:, None]
    phases = (shifts * orders % samples).astype(jnp.float32) * (2.0 * jnp.pi / samples)
    cosine = jnp.cos(phases)
    sine_part = jnp.sin(phases)
    real_part = own[..., :bin_count].astype(jnp.float32)[..., None, :]
    imag_part = own[..., bin_count:].astype(jnp.float32)[..., None, :]
    back_real = real_part * cosine - imag_part * sine_part
    back_imag = imag_part * cosine + real_part * sine_part
    return jnp.concatenate([back_real, back_imag], axis=-1).astype(jnp.bfloat16)


def diagonal_band(matrix, offsets):
    row_count, col_count = matrix.shape
    flat_rows = matrix.reshape(row_count * col_count)
    padded = jnp.concatenate([flat_rows, jnp.zeros((row_count,), matrix.dtype)])
    skewed = padded.reshape(row_count, col_count + 1)
    return skewed[:, :offsets]


def band_weights(pair_counts, band_lows, band_highs, bin_count):
    offsets = jnp.arange(pair_counts.shape[1], dtype=jnp.int32)[None, :]
    in_band = (offsets >= band_lows[:, None]) & (offsets < band_highs[:, None])
    return jnp.where(
        in_band, 1.0 / jnp.sqrt(float(bin_count) * jnp.maximum(pair_counts, 1.0)), 0.0
    )


def band_kernel(block_ref, weight_ref, out_ref):
    width = out_ref.shape[2]
    lanes = block_ref.shape[2]
    for row in range(out_ref.shape[0]):
        lagged = pltpu.roll(block_ref[row], (lanes - row) % lanes, 1)[:, :width]
        out_ref[row] = lagged * weight_ref[row : row + 1, :]


def band_of(block, weights):
    rows, lags, _ = block.shape
    width = weights.shape[1]
    return pl.pallas_call(
        band_kernel,
        out_shape=jax.ShapeDtypeStruct((rows, lags, width), jnp.float32),
        in_specs=[pl.BlockSpec(memory_space=pltpu.VMEM)] * 2,
        out_specs=pl.BlockSpec(memory_space=pltpu.VMEM),
    )(block, weights)


def pack_kernel(raw_ref, out_ref, pad_ref):
    rows, width = raw_ref.shape[1], raw_ref.shape[2]
    half, lanes = out_ref.shape[1], out_ref.shape[2]
    pad_ref[...] = jnp.zeros(pad_ref.shape, jnp.float32)
    pad_ref[:rows] = raw_ref[0].astype(jnp.float32)
    top, bottom = pad_ref[:half], pad_ref[half:]
    low = lax.broadcasted_iota(jnp.int32, top.shape, 1) % lanes < lanes // 2
    even = jnp.where(low, top, pltpu.roll(bottom, lanes // 2, 1)).astype(out_ref.dtype)
    odd = jnp.where(low, pltpu.roll(top, width - lanes // 2, 1), bottom).astype(out_ref.dtype)
    for tile in range(out_ref.shape[0] // 2):
        out_ref[2 * tile] = even[:, tile * lanes : (tile + 1) * lanes]
        out_ref[2 * tile + 1] = odd[:, tile * lanes : (tile + 1) * lanes]


def pack(raw_strain, half, tiles_per_step=8):
    _, rows, channels = raw_strain.shape
    lanes = 128
    tiles = channels // lanes
    return pl.pallas_call(
        pack_kernel,
        out_shape=jax.ShapeDtypeStruct((2 * tiles, half, lanes), raw_strain.dtype),
        grid=(tiles // tiles_per_step,),
        in_specs=[pl.BlockSpec((1, rows, tiles_per_step * lanes), lambda i: (0, 0, i))],
        out_specs=pl.BlockSpec((2 * tiles_per_step, half, lanes), lambda i: (i, 0, 0)),
        scratch_shapes=[pltpu.VMEM((2 * half, tiles_per_step * lanes), jnp.float32)],
    )(raw_strain)


def local(raw_strain, window_valid, band_first, band_end):
    n_ch = lax.axis_size("ch")
    n_grp = lax.axis_size("grp")
    _, t_here, channels = raw_strain.shape
    per_dev = channels // n_ch
    pair_width = 2 * per_dev
    half = ((t_here + 1) // 2 + 15) // 16 * 16
    me = lax.axis_index("ch")
    side = me % 2

    samples = pack(raw_strain, half)
    samples = lax.all_to_all(samples, "ch", 0, 0, tiled=True)
    samples = samples.reshape(n_ch, half, 2, per_dev)

    block_starts = jnp.arange(n_ch, dtype=jnp.int32) * t_here
    offsets = jnp.arange(2 * half, dtype=jnp.int32)
    table = dft_rows(block_starts, offsets, NT, F).reshape(n_ch, 2, half, 2 * F)
    spectra = jnp.einsum("srhc,shrf->cf", samples, table, preferred_element_type=jnp.float32)

    whitened = whiten(spectra, F, SMOOTH)
    valid_flags = window_valid.astype(jnp.bfloat16)
    group_index = lax.axis_index("grp")
    own_flags = lax.dynamic_slice_in_dim(valid_flags, group_index, 1, 0)
    whitened = whitened * own_flags[0][:, None]
    blocks_up = (KH + per_dev - 1) // per_dev
    own_rows = jnp.broadcast_to(whitened[None], (n_grp,) + whitened.shape)
    own_rows = lax.all_to_all(own_rows, "grp", 0, 0, tiled=True)
    white_parts = [own_rows]
    flag_parts = [valid_flags]
    for neighbour in range(1, blocks_up + 1):
        moved_white, moved_flags = from_behind((own_rows, valid_flags), "ch", -neighbour)
        white_parts.append(moved_white)
        flag_parts.append(moved_flags)
    rows_used = per_dev * (blocks_up + 1)
    lanes = 128 * pl.cdiv(rows_used, 128)
    white_parts.append(jnp.zeros((n_grp, lanes - rows_used, 2 * F), jnp.bfloat16))
    windows = jnp.concatenate(white_parts, axis=1)
    ext_flags = jnp.concatenate(flag_parts, axis=1)

    pair_full = jnp.einsum("na,nb->ab", valid_flags, ext_flags, preferred_element_type=jnp.float32)
    pair_counts = diagonal_band(pair_full, KH)
    turned = unturned(own_rows, -(LAGS // 2), LAGS, LAG_STEP, NT, F)
    block = jnp.einsum("walj,wbj->alb", turned, windows, preferred_element_type=jnp.float32)
    weights = band_weights(pair_counts, band_first, band_end, F)
    return band_of(block, weights)


def solution(mesh):
    placed = (P("grp", "ch", None), P(None, "ch"), P("ch"), P("ch"))
    return jax.shard_map(
        local, mesh=mesh, in_specs=placed, out_specs=P("ch", None, None), check_vma=False
    )
```

```python
import jax
import jax.numpy as jnp
from jax import lax
from jax.experimental import pallas as pl
from jax.experimental.pallas import tpu as pltpu
from jax.sharding import PartitionSpec as P


NT = 7680
F = 384
KH = 128
SMOOTH = 65
LAGS = 32
LAG_STEP = 10


eps_white = 1e-06


def from_behind(array, axis, by):
    count = lax.axis_size(axis)
    pairs = [(i, i + by) for i in range(count) if 0 <= i + by < count]
    return lax.ppermute(array, axis, pairs)


def smoothing_matrix(bin_count, window_bins):
    row_index = jnp.arange(bin_count, dtype=jnp.int32)[:, None]
    col_index = jnp.arange(bin_count, dtype=jnp.int32)[None, :]
    distance = (row_index - col_index) % bin_count
    halfwidth = window_bins // 2
    inside = (distance <= halfwidth) | (distance >= bin_count - halfwidth)
    return inside.astype(jnp.float32)


def whiten(spectra, bin_count, window_bins):
    real_part = spectra[..., :bin_count]
    imag_part = spectra[..., bin_count:]
    magnitude = jnp.sqrt(real_part * real_part + imag_part * imag_part)
    averaged = (
        jnp.dot(
            magnitude,
            smoothing_matrix(bin_count, window_bins),
            precision=lax.Precision.HIGHEST,
            preferred_element_type=jnp.float32,
        )
        / window_bins
    )
    factor = 1.0 / (averaged + eps_white)
    return (spectra * jnp.concatenate([factor, factor], axis=-1)).astype(jnp.bfloat16)


def phase_of(index, samples):
    return (index % samples).astype(jnp.float32) * (2.0 * jnp.pi / samples)


def dft_rows(block_starts, offsets, samples, bin_count):
    orders = jnp.arange(1, bin_count + 1, dtype=jnp.int32)[None, :]
    outer = phase_of(block_starts[:, None] * orders, samples)
    inner = phase_of(offsets[:, None] * orders, samples)
    outer_cos, outer_sin = jnp.cos(outer)[:, None, :], jnp.sin(outer)[:, None, :]
    inner_cos, inner_sin = jnp.cos(inner)[None, :, :], jnp.sin(inner)[None, :, :]
    cosine = outer_cos * inner_cos - outer_sin * inner_sin
    sine_part = outer_sin * inner_cos + outer_cos * inner_sin
    table = jnp.concatenate([cosine, -sine_part], axis=-1)
    return table.reshape(-1, 2 * bin_count).astype(jnp.bfloat16)


def unturned(own, lag_first, lag_count, lag_step, samples, bin_count):
    orders = jnp.arange(1, bin_count + 1, dtype=jnp.int32)[None, :]
    shifts = ((lag_first + jnp.arange(lag_count, dtype=jnp.int32)) * lag_step)[:, None]
    phases = (shifts * orders % samples).astype(jnp.float32) * (2.0 * jnp.pi / samples)
    cosine = jnp.cos(phases)
    sine_part = jnp.sin(phases)
    real_part = own[..., :bin_count].astype(jnp.float32)[..., None, :]
    imag_part = own[..., bin_count:].astype(jnp.float32)[..., None, :]
    back_real = real_part * cosine - imag_part * sine_part
    back_imag = imag_part * cosine + real_part * sine_part
    return jnp.concatenate([back_real, back_imag], axis=-1).astype(jnp.bfloat16)


def diagonal_band(matrix, offsets):
    row_count, col_count = matrix.shape
    flat_rows = matrix.reshape(row_count * col_count)
    padded = jnp.concatenate([flat_rows, jnp.zeros((row_count,), matrix.dtype)])
    skewed = padded.reshape(row_count, col_count + 1)
    return skewed[:, :offsets]


def band_weights(pair_counts, band_lows, band_highs, bin_count):
    offsets = jnp.arange(pair_counts.shape[1], dtype=jnp.int32)[None, :]
    in_band = (offsets >= band_lows[:, None]) & (offsets < band_highs[:, None])
    return jnp.where(
        in_band, 1.0 / jnp.sqrt(float(bin_count) * jnp.maximum(pair_counts, 1.0)), 0.0
    )


def band_kernel(block_ref, weight_ref, out_ref):
    width = out_ref.shape[2]
    lanes = block_ref.shape[2]
    for row in range(out_ref.shape[0]):
        lagged = pltpu.roll(block_ref[row], (lanes - row) % lanes, 1)[:, :width]
        out_ref[row] = lagged * weight_ref[row : row + 1, :]


def band_of(block, weights):
    rows, lags, _ = block.shape
    width = weights.shape[1]
    return pl.pallas_call(
        band_kernel,
        out_shape=jax.ShapeDtypeStruct((rows, lags, width), jnp.float32),
        in_specs=[pl.BlockSpec(memory_space=pltpu.VMEM)] * 2,
        out_specs=pl.BlockSpec(memory_space=pltpu.VMEM),
    )(block, weights)


def pack_kernel(raw_ref, out_ref, pad_ref):
    rows, width = raw_ref.shape[1], raw_ref.shape[2]
    half, lanes = out_ref.shape[1], out_ref.shape[2]
    pad_ref[...] = jnp.zeros(pad_ref.shape, jnp.float32)
    pad_ref[:rows] = raw_ref[0].astype(jnp.float32)
    top, bottom = pad_ref[:half], pad_ref[half:]
    low = lax.broadcasted_iota(jnp.int32, top.shape, 1) % lanes < lanes // 2
    even = jnp.where(low, top, pltpu.roll(bottom, lanes // 2, 1)).astype(out_ref.dtype)
    odd = jnp.where(low, pltpu.roll(top, width - lanes // 2, 1), bottom).astype(out_ref.dtype)
    for tile in range(out_ref.shape[0] // 2):
        out_ref[2 * tile] = even[:, tile * lanes : (tile + 1) * lanes]
        out_ref[2 * tile + 1] = odd[:, tile * lanes : (tile + 1) * lanes]


def pack(raw_strain, half, tiles_per_step=32):
    _, rows, channels = raw_strain.shape
    lanes = 128
    tiles = channels // lanes
    return pl.pallas_call(
        pack_kernel,
        out_shape=jax.ShapeDtypeStruct((2 * tiles, half, lanes), raw_strain.dtype),
        grid=(tiles // tiles_per_step,),
        in_specs=[pl.BlockSpec((1, rows, tiles_per_step * lanes), lambda i: (0, 0, i))],
        out_specs=pl.BlockSpec((2 * tiles_per_step, half, lanes), lambda i: (i, 0, 0)),
        scratch_shapes=[pltpu.VMEM((2 * half, tiles_per_step * lanes), jnp.float32)],
    )(raw_strain)


def local(raw_strain, window_valid, band_first, band_end):
    n_ch = lax.axis_size("ch")
    n_grp = lax.axis_size("grp")
    _, t_here, channels = raw_strain.shape
    per_dev = channels // n_ch
    pair_width = 2 * per_dev
    half = ((t_here + 1) // 2 + 15) // 16 * 16
    me = lax.axis_index("ch")
    side = me % 2

    samples = pack(raw_strain, half)
    samples = lax.all_to_all(samples, "ch", 0, 0, tiled=True)
    samples = samples.reshape(n_ch * half, 2 * per_dev)

    block_starts = jnp.arange(n_ch, dtype=jnp.int32) * t_here
    offsets = jnp.arange(2 * half, dtype=jnp.int32)
    table = dft_rows(block_starts, offsets, NT, F).reshape(n_ch, 2, half, 2 * F)
    table = table.transpose(0, 2, 1, 3).reshape(n_ch * half, 2 * 2 * F)
    both = jnp.einsum("tc,tf->cf", samples, table, preferred_element_type=jnp.float32)
    spectra = both[:per_dev, : 2 * F] + both[per_dev:, 2 * F :]

    whitened = whiten(spectra, F, SMOOTH)
    valid_flags = window_valid.astype(jnp.bfloat16)
    group_index = lax.axis_index("grp")
    own_flags = lax.dynamic_slice_in_dim(valid_flags, group_index, 1, 0)
    whitened = whitened * own_flags[0][:, None]
    blocks_up = (KH + per_dev - 1) // per_dev
    own_rows = jnp.broadcast_to(whitened[None], (n_grp,) + whitened.shape)
    own_rows = lax.all_to_all(own_rows, "grp", 0, 0, tiled=True)
    white_parts = [own_rows]
    flag_parts = [valid_flags]
    for neighbour in range(1, blocks_up + 1):
        moved_white, moved_flags = from_behind((own_rows, valid_flags), "ch", -neighbour)
        white_parts.append(moved_white)
        flag_parts.append(moved_flags)
    rows_used = per_dev * (blocks_up + 1)
    lanes = 128 * pl.cdiv(rows_used, 128)
    white_parts.append(jnp.zeros((n_grp, lanes - rows_used, 2 * F), jnp.bfloat16))
    windows = jnp.concatenate(white_parts, axis=1)
    ext_flags = jnp.concatenate(flag_parts, axis=1)

    pair_full = jnp.einsum("na,nb->ab", valid_flags, ext_flags, preferred_element_type=jnp.float32)
    pair_counts = diagonal_band(pair_full, KH)
    turned = unturned(own_rows, -(LAGS // 2), LAGS, LAG_STEP, NT, F)
    block = jnp.einsum("walj,wbj->alb", turned, windows, preferred_element_type=jnp.float32)
    weights = band_weights(pair_counts, band_first, band_end, F)
    return band_of(block, weights)


def solution(mesh):
    placed = (P("grp", "ch", None), P(None, "ch"), P("ch"), P("ch"))
    return jax.shard_map(
        local, mesh=mesh, in_specs=placed, out_specs=P("ch", None, None), check_vma=False
    )
```

```python
import jax
import jax.numpy as jnp
from jax import lax
from jax.experimental import pallas as pl
from jax.experimental.pallas import tpu as pltpu
from jax.sharding import PartitionSpec as P


NT = 7680
F = 384
KH = 128
SMOOTH = 65
LAGS = 32
LAG_STEP = 10


eps_white = 1e-06


def from_behind(array, axis, by):
    count = lax.axis_size(axis)
    pairs = [(i, i + by) for i in range(count) if 0 <= i + by < count]
    return lax.ppermute(array, axis, pairs)


def smoothing_matrix(bin_count, window_bins):
    row_index = jnp.arange(bin_count, dtype=jnp.int32)[:, None]
    col_index = jnp.arange(bin_count, dtype=jnp.int32)[None, :]
    distance = (row_index - col_index) % bin_count
    halfwidth = window_bins // 2
    inside = (distance <= halfwidth) | (distance >= bin_count - halfwidth)
    return inside.astype(jnp.float32)


def whiten(spectra, bin_count, window_bins):
    real_part = spectra[..., :bin_count]
    imag_part = spectra[..., bin_count:]
    magnitude = jnp.sqrt(real_part * real_part + imag_part * imag_part)
    averaged = (
        jnp.dot(
            magnitude,
            smoothing_matrix(bin_count, window_bins),
            precision=lax.Precision.HIGHEST,
            preferred_element_type=jnp.float32,
        )
        / window_bins
    )
    factor = 1.0 / (averaged + eps_white)
    return (spectra * jnp.concatenate([factor, factor], axis=-1)).astype(jnp.bfloat16)


def phase_of(index, samples):
    return (index % samples).astype(jnp.float32) * (2.0 * jnp.pi / samples)


def dft_rows(block_starts, offsets, samples, bin_count):
    orders = jnp.arange(1, bin_count + 1, dtype=jnp.int32)[None, :]
    outer = phase_of(block_starts[:, None] * orders, samples)
    inner = phase_of(offsets[:, None] * orders, samples)
    outer_cos, outer_sin = jnp.cos(outer)[:, None, :], jnp.sin(outer)[:, None, :]
    inner_cos, inner_sin = jnp.cos(inner)[None, :, :], jnp.sin(inner)[None, :, :]
    cosine = outer_cos * inner_cos - outer_sin * inner_sin
    sine_part = outer_sin * inner_cos + outer_cos * inner_sin
    table = jnp.concatenate([cosine, -sine_part], axis=-1)
    return table.reshape(-1, 2 * bin_count).astype(jnp.bfloat16)


def unturned(own, lag_first, lag_count, lag_step, samples, bin_count):
    orders = jnp.arange(1, bin_count + 1, dtype=jnp.int32)[None, :]
    shifts = ((lag_first + jnp.arange(lag_count, dtype=jnp.int32)) * lag_step)[:, None]
    phases = (shifts * orders % samples).astype(jnp.float32) * (2.0 * jnp.pi / samples)
    cosine = jnp.cos(phases)
    sine_part = jnp.sin(phases)
    real_part = own[..., :bin_count].astype(jnp.float32)[..., None, :]
    imag_part = own[..., bin_count:].astype(jnp.float32)[..., None, :]
    back_real = real_part * cosine - imag_part * sine_part
    back_imag = imag_part * cosine + real_part * sine_part
    return jnp.concatenate([back_real, back_imag], axis=-1).astype(jnp.bfloat16)


def diagonal_band(matrix, offsets):
    row_count, col_count = matrix.shape
    flat_rows = matrix.reshape(row_count * col_count)
    padded = jnp.concatenate([flat_rows, jnp.zeros((row_count,), matrix.dtype)])
    skewed = padded.reshape(row_count, col_count + 1)
    return skewed[:, :offsets]


def band_weights(pair_counts, band_lows, band_highs, bin_count):
    offsets = jnp.arange(pair_counts.shape[1], dtype=jnp.int32)[None, :]
    in_band = (offsets >= band_lows[:, None]) & (offsets < band_highs[:, None])
    return jnp.where(
        in_band, 1.0 / jnp.sqrt(float(bin_count) * jnp.maximum(pair_counts, 1.0)), 0.0
    )


def band_kernel(block_ref, weight_ref, out_ref):
    width = out_ref.shape[2]
    lanes = block_ref.shape[2]
    for row in range(out_ref.shape[0]):
        lagged = pltpu.roll(block_ref[row], (lanes - row) % lanes, 1)[:, :width]
        out_ref[row] = lagged * weight_ref[row : row + 1, :]


def band_of(block, weights):
    rows, lags, _ = block.shape
    width = weights.shape[1]
    return pl.pallas_call(
        band_kernel,
        out_shape=jax.ShapeDtypeStruct((rows, lags, width), jnp.float32),
        in_specs=[pl.BlockSpec(memory_space=pltpu.VMEM)] * 2,
        out_specs=pl.BlockSpec(memory_space=pltpu.VMEM),
    )(block, weights)


def pack_kernel(raw_ref, out_ref, pad_ref):
    rows, width = raw_ref.shape[1], raw_ref.shape[2]
    half, lanes = out_ref.shape[1], out_ref.shape[2]
    pad_ref[...] = jnp.zeros(pad_ref.shape, jnp.float32)
    pad_ref[:rows] = raw_ref[0].astype(jnp.float32)
    top, bottom = pad_ref[:half], pad_ref[half:]
    low = lax.broadcasted_iota(jnp.int32, top.shape, 1) % lanes < lanes // 2
    even = jnp.where(low, top, pltpu.roll(bottom, lanes // 2, 1)).astype(out_ref.dtype)
    odd = jnp.where(low, pltpu.roll(top, width - lanes // 2, 1), bottom).astype(out_ref.dtype)
    for tile in range(out_ref.shape[0] // 2):
        out_ref[2 * tile] = even[:, tile * lanes : (tile + 1) * lanes]
        out_ref[2 * tile + 1] = odd[:, tile * lanes : (tile + 1) * lanes]


def pack(raw_strain, half, tiles_per_step=32):
    _, rows, channels = raw_strain.shape
    lanes = 128
    tiles = channels // lanes
    return pl.pallas_call(
        pack_kernel,
        out_shape=jax.ShapeDtypeStruct((2 * tiles, half, lanes), raw_strain.dtype),
        grid=(tiles // tiles_per_step,),
        in_specs=[pl.BlockSpec((1, rows, tiles_per_step * lanes), lambda i: (0, 0, i))],
        out_specs=pl.BlockSpec((2 * tiles_per_step, half, lanes), lambda i: (i, 0, 0)),
        scratch_shapes=[pltpu.VMEM((2 * half, tiles_per_step * lanes), jnp.float32)],
    )(raw_strain)


def local(raw_strain, window_valid, band_first, band_end):
    n_ch = lax.axis_size("ch")
    n_grp = lax.axis_size("grp")
    _, t_here, channels = raw_strain.shape
    per_dev = channels // n_ch
    pair_width = 2 * per_dev
    half = ((t_here + 1) // 2 + 15) // 16 * 16
    me = lax.axis_index("ch")
    side = me % 2

    samples = pack(raw_strain, half)
    samples, window_valid = lax.optimization_barrier((samples, window_valid))
    samples = lax.all_to_all(samples, "ch", 0, 0, tiled=True)
    samples = samples.reshape(n_ch, half, 2, per_dev)

    block_starts = jnp.arange(n_ch, dtype=jnp.int32) * t_here
    offsets = jnp.arange(2 * half, dtype=jnp.int32)
    table = dft_rows(block_starts, offsets, NT, F).reshape(n_ch, 2, half, 2 * F)
    spectra = jnp.einsum("srhc,shrf->cf", samples, table, preferred_element_type=jnp.float32)

    whitened = whiten(spectra, F, SMOOTH)
    valid_flags = window_valid.astype(jnp.bfloat16)
    group_index = lax.axis_index("grp")
    own_flags = lax.dynamic_slice_in_dim(valid_flags, group_index, 1, 0)
    whitened = whitened * own_flags[0][:, None]
    blocks_up = (KH + per_dev - 1) // per_dev
    own_rows = jnp.broadcast_to(whitened[None], (n_grp,) + whitened.shape)
    own_rows = lax.all_to_all(own_rows, "grp", 0, 0, tiled=True)
    white_parts = [own_rows]
    flag_parts = [valid_flags]
    for neighbour in range(1, blocks_up + 1):
        moved_white, moved_flags = from_behind((own_rows, valid_flags), "ch", -neighbour)
        white_parts.append(moved_white)
        flag_parts.append(moved_flags)
    rows_used = per_dev * (blocks_up + 1)
    lanes = 128 * pl.cdiv(rows_used, 128)
    white_parts.append(jnp.zeros((n_grp, lanes - rows_used, 2 * F), jnp.bfloat16))
    windows = jnp.concatenate(white_parts, axis=1)
    ext_flags = jnp.concatenate(flag_parts, axis=1)

    pair_full = jnp.einsum("na,nb->ab", valid_flags, ext_flags, preferred_element_type=jnp.float32)
    pair_counts = diagonal_band(pair_full, KH)
    turned = unturned(own_rows, -(LAGS // 2), LAGS, LAG_STEP, NT, F)
    block = jnp.einsum("walj,wbj->alb", turned, windows, preferred_element_type=jnp.float32)
    weights = band_weights(pair_counts, band_first, band_end, F)
    return band_of(block, weights)


def solution(mesh):
    placed = (P("grp", "ch", None), P(None, "ch"), P("ch"), P("ch"))
    return jax.shard_map(
        local, mesh=mesh, in_specs=placed, out_specs=P("ch", None, None), check_vma=False
    )
```

```python
import jax
import jax.numpy as jnp
from jax import lax
from jax.experimental import pallas as pl
from jax.experimental.pallas import tpu as pltpu
from jax.sharding import PartitionSpec as P


NT = 7680
F = 384
KH = 128
SMOOTH = 65
LAGS = 32
LAG_STEP = 10


eps_white = 1e-06


def from_behind(array, axis, by):
    count = lax.axis_size(axis)
    pairs = [(i, i + by) for i in range(count) if 0 <= i + by < count]
    return lax.ppermute(array, axis, pairs)


def smoothing_matrix(bin_count, window_bins):
    row_index = jnp.arange(bin_count, dtype=jnp.int32)[:, None]
    col_index = jnp.arange(bin_count, dtype=jnp.int32)[None, :]
    distance = (row_index - col_index) % bin_count
    halfwidth = window_bins // 2
    inside = (distance <= halfwidth) | (distance >= bin_count - halfwidth)
    return inside.astype(jnp.float32)


def whiten(spectra, bin_count, window_bins):
    real_part = spectra[..., :bin_count]
    imag_part = spectra[..., bin_count:]
    magnitude = jnp.sqrt(real_part * real_part + imag_part * imag_part)
    averaged = (
        jnp.dot(
            magnitude,
            smoothing_matrix(bin_count, window_bins),
            precision=lax.Precision.HIGHEST,
            preferred_element_type=jnp.float32,
        )
        / window_bins
    )
    factor = 1.0 / (averaged + eps_white)
    return (spectra * jnp.concatenate([factor, factor], axis=-1)).astype(jnp.bfloat16)


def phase_of(index, samples):
    return (index % samples).astype(jnp.float32) * (2.0 * jnp.pi / samples)


def dft_rows(block_starts, offsets, samples, bin_count):
    orders = jnp.arange(1, bin_count + 1, dtype=jnp.int32)[None, :]
    outer = phase_of(block_starts[:, None] * orders, samples)
    inner = phase_of(offsets[:, None] * orders, samples)
    outer_cos, outer_sin = jnp.cos(outer)[:, None, :], jnp.sin(outer)[:, None, :]
    inner_cos, inner_sin = jnp.cos(inner)[None, :, :], jnp.sin(inner)[None, :, :]
    cosine = outer_cos * inner_cos - outer_sin * inner_sin
    sine_part = outer_sin * inner_cos + outer_cos * inner_sin
    table = jnp.concatenate([cosine, -sine_part], axis=-1)
    return table.reshape(-1, 2 * bin_count).astype(jnp.bfloat16)


def unturned(own, lag_first, lag_count, lag_step, samples, bin_count):
    orders = jnp.arange(1, bin_count + 1, dtype=jnp.int32)[None, :]
    shifts = ((lag_first + jnp.arange(lag_count, dtype=jnp.int32)) * lag_step)[:, None]
    phases = (shifts * orders % samples).astype(jnp.float32) * (2.0 * jnp.pi / samples)
    cosine = jnp.cos(phases)
    sine_part = jnp.sin(phases)
    real_part = own[..., :bin_count].astype(jnp.float32)[..., None, :]
    imag_part = own[..., bin_count:].astype(jnp.float32)[..., None, :]
    back_real = real_part * cosine - imag_part * sine_part
    back_imag = imag_part * cosine + real_part * sine_part
    return jnp.concatenate([back_real, back_imag], axis=-1).astype(jnp.bfloat16)


def diagonal_band(matrix, offsets):
    row_count, col_count = matrix.shape
    flat_rows = matrix.reshape(row_count * col_count)
    padded = jnp.concatenate([flat_rows, jnp.zeros((row_count,), matrix.dtype)])
    skewed = padded.reshape(row_count, col_count + 1)
    return skewed[:, :offsets]


def band_weights(pair_counts, band_lows, band_highs, bin_count):
    offsets = jnp.arange(pair_counts.shape[1], dtype=jnp.int32)[None, :]
    in_band = (offsets >= band_lows[:, None]) & (offsets < band_highs[:, None])
    return jnp.where(
        in_band, 1.0 / jnp.sqrt(float(bin_count) * jnp.maximum(pair_counts, 1.0)), 0.0
    )


def band_kernel(near_ref, far_ref, weight_ref, out_ref):
    width = out_ref.shape[2]
    lanes = near_ref.shape[2] + far_ref.shape[2]
    for row in range(out_ref.shape[0]):
        block = jnp.concatenate([near_ref[row], far_ref[row]], axis=1)
        lagged = pltpu.roll(block, (lanes - row) % lanes, 1)[:, :width]
        out_ref[row] = lagged * weight_ref[row : row + 1, :]


def band_of(near, far, weights):
    rows, lags, _ = near.shape
    width = weights.shape[1]
    return pl.pallas_call(
        band_kernel,
        out_shape=jax.ShapeDtypeStruct((rows, lags, width), jnp.float32),
        in_specs=[pl.BlockSpec(memory_space=pltpu.VMEM)] * 3,
        out_specs=pl.BlockSpec(memory_space=pltpu.VMEM),
    )(near, far, weights)


def pack_kernel(raw_ref, out_ref, pad_ref):
    rows, width = raw_ref.shape[1], raw_ref.shape[2]
    half, lanes = out_ref.shape[1], out_ref.shape[2]
    pad_ref[...] = jnp.zeros(pad_ref.shape, jnp.float32)
    pad_ref[:rows] = raw_ref[0].astype(jnp.float32)
    top, bottom = pad_ref[:half], pad_ref[half:]
    low = lax.broadcasted_iota(jnp.int32, top.shape, 1) % lanes < lanes // 2
    even = jnp.where(low, top, pltpu.roll(bottom, lanes // 2, 1)).astype(out_ref.dtype)
    odd = jnp.where(low, pltpu.roll(top, width - lanes // 2, 1), bottom).astype(out_ref.dtype)
    for tile in range(out_ref.shape[0] // 2):
        out_ref[2 * tile] = even[:, tile * lanes : (tile + 1) * lanes]
        out_ref[2 * tile + 1] = odd[:, tile * lanes : (tile + 1) * lanes]


def pack(raw_strain, half, tiles_per_step=32):
    _, rows, channels = raw_strain.shape
    lanes = 128
    tiles = channels // lanes
    return pl.pallas_call(
        pack_kernel,
        out_shape=jax.ShapeDtypeStruct((2 * tiles, half, lanes), raw_strain.dtype),
        grid=(tiles // tiles_per_step,),
        in_specs=[pl.BlockSpec((1, rows, tiles_per_step * lanes), lambda i: (0, 0, i))],
        out_specs=pl.BlockSpec((2 * tiles_per_step, half, lanes), lambda i: (i, 0, 0)),
        scratch_shapes=[pltpu.VMEM((2 * half, tiles_per_step * lanes), jnp.float32)],
    )(raw_strain)


def local(raw_strain, window_valid, band_first, band_end):
    n_ch = lax.axis_size("ch")
    n_grp = lax.axis_size("grp")
    _, t_here, channels = raw_strain.shape
    per_dev = channels // n_ch
    pair_width = 2 * per_dev
    half = ((t_here + 1) // 2 + 15) // 16 * 16
    me = lax.axis_index("ch")
    side = me % 2

    samples = pack(raw_strain, half)
    samples, window_valid = lax.optimization_barrier((samples, window_valid))
    samples = lax.all_to_all(samples, "ch", 0, 0, tiled=True)
    samples = samples.reshape(n_ch, half, 2, per_dev)

    block_starts = jnp.arange(n_ch, dtype=jnp.int32) * t_here
    offsets = jnp.arange(2 * half, dtype=jnp.int32)
    table = dft_rows(block_starts, offsets, NT, F).reshape(n_ch, 2, half, 2 * F)
    spectra = jnp.einsum("srhc,shrf->cf", samples, table, preferred_element_type=jnp.float32)

    whitened = whiten(spectra, F, SMOOTH)
    valid_flags = window_valid.astype(jnp.bfloat16)
    group_index = lax.axis_index("grp")
    own_flags = lax.dynamic_slice_in_dim(valid_flags, group_index, 1, 0)
    whitened = whitened * own_flags[0][:, None]
    blocks_up = (KH + per_dev - 1) // per_dev
    own_rows = jnp.broadcast_to(whitened[None], (n_grp,) + whitened.shape)
    own_rows = lax.all_to_all(own_rows, "grp", 0, 0, tiled=True)
    white_parts = [own_rows]
    flag_parts = [valid_flags]
    for neighbour in range(1, blocks_up + 1):
        moved_white, moved_flags = from_behind((own_rows, valid_flags), "ch", -neighbour)
        white_parts.append(moved_white)
        flag_parts.append(moved_flags)
    rows_used = per_dev * (blocks_up + 1)
    lanes = 128 * pl.cdiv(rows_used, 128)
    white_parts.append(jnp.zeros((n_grp, lanes - rows_used, 2 * F), jnp.bfloat16))
    near = jnp.concatenate(white_parts[:2], axis=1)
    far = jnp.concatenate(white_parts[2:], axis=1)
    ext_flags = jnp.concatenate(flag_parts, axis=1)

    pair_full = jnp.einsum("na,nb->ab", valid_flags, ext_flags, preferred_element_type=jnp.float32)
    pair_counts = diagonal_band(pair_full, KH)
    turned = unturned(own_rows, -(LAGS // 2), LAGS, LAG_STEP, NT, F)
    near = jnp.einsum("walj,wbj->alb", turned, near, preferred_element_type=jnp.float32)
    far = jnp.einsum("walj,wbj->alb", turned, far, preferred_element_type=jnp.float32)
    weights = band_weights(pair_counts, band_first, band_end, F)
    return band_of(near, far, weights)


def solution(mesh):
    placed = (P("grp", "ch", None), P(None, "ch"), P("ch"), P("ch"))
    return jax.shard_map(
        local, mesh=mesh, in_specs=placed, out_specs=P("ch", None, None), check_vma=False
    )
```

```python
import jax
import jax.numpy as jnp
from jax import lax
from jax.experimental import pallas as pl
from jax.experimental.pallas import tpu as pltpu
from jax.sharding import PartitionSpec as P


NT = 7680
F = 384
KH = 128
SMOOTH = 65
LAGS = 32
LAG_STEP = 10


eps_white = 1e-06


def from_behind(array, axis, by):
    count = lax.axis_size(axis)
    pairs = [(i, i + by) for i in range(count) if 0 <= i + by < count]
    return lax.ppermute(array, axis, pairs)


def smoothing_matrix(bin_count, window_bins):
    row_index = jnp.arange(bin_count, dtype=jnp.int32)[:, None]
    col_index = jnp.arange(bin_count, dtype=jnp.int32)[None, :]
    distance = (row_index - col_index) % bin_count
    halfwidth = window_bins // 2
    inside = (distance <= halfwidth) | (distance >= bin_count - halfwidth)
    return inside.astype(jnp.float32)


def whiten(spectra, bin_count, window_bins):
    real_part = spectra[..., :bin_count]
    imag_part = spectra[..., bin_count:]
    magnitude = jnp.sqrt(real_part * real_part + imag_part * imag_part)
    averaged = (
        jnp.dot(
            magnitude,
            smoothing_matrix(bin_count, window_bins),
            precision=lax.Precision.HIGHEST,
            preferred_element_type=jnp.float32,
        )
        / window_bins
    )
    factor = 1.0 / (averaged + eps_white)
    return (spectra * jnp.concatenate([factor, factor], axis=-1)).astype(jnp.bfloat16)


def phase_of(index, samples):
    return (index % samples).astype(jnp.float32) * (2.0 * jnp.pi / samples)


def dft_rows(block_starts, offsets, samples, bin_count):
    orders = jnp.arange(1, bin_count + 1, dtype=jnp.int32)[None, :]
    outer = phase_of(block_starts[:, None] * orders, samples)
    inner = phase_of(offsets[:, None] * orders, samples)
    outer_cos, outer_sin = jnp.cos(outer)[:, None, :], jnp.sin(outer)[:, None, :]
    inner_cos, inner_sin = jnp.cos(inner)[None, :, :], jnp.sin(inner)[None, :, :]
    cosine = outer_cos * inner_cos - outer_sin * inner_sin
    sine_part = outer_sin * inner_cos + outer_cos * inner_sin
    table = jnp.concatenate([cosine, -sine_part], axis=-1)
    return table.reshape(-1, 2 * bin_count).astype(jnp.bfloat16)


def unturned(own, lag_first, lag_count, lag_step, samples, bin_count):
    orders = jnp.arange(1, bin_count + 1, dtype=jnp.int32)[None, :]
    shifts = ((lag_first + jnp.arange(lag_count, dtype=jnp.int32)) * lag_step)[:, None]
    phases = (shifts * orders % samples).astype(jnp.float32) * (2.0 * jnp.pi / samples)
    cosine = jnp.cos(phases)
    sine_part = jnp.sin(phases)
    real_part = own[..., :bin_count].astype(jnp.float32)[..., None, :]
    imag_part = own[..., bin_count:].astype(jnp.float32)[..., None, :]
    back_real = real_part * cosine - imag_part * sine_part
    back_imag = imag_part * cosine + real_part * sine_part
    return jnp.concatenate([back_real, back_imag], axis=-1).astype(jnp.bfloat16)


def diagonal_band(matrix, offsets):
    row_count, col_count = matrix.shape
    flat_rows = matrix.reshape(row_count * col_count)
    padded = jnp.concatenate([flat_rows, jnp.zeros((row_count,), matrix.dtype)])
    skewed = padded.reshape(row_count, col_count + 1)
    return skewed[:, :offsets]


def band_weights(pair_counts, band_lows, band_highs, bin_count):
    offsets = jnp.arange(pair_counts.shape[1], dtype=jnp.int32)[None, :]
    in_band = (offsets >= band_lows[:, None]) & (offsets < band_highs[:, None])
    return jnp.where(
        in_band, 1.0 / jnp.sqrt(float(bin_count) * jnp.maximum(pair_counts, 1.0)), 0.0
    )


def band_kernel(near_ref, far_ref, weight_ref, out_ref):
    rows, width = out_ref.shape[0], out_ref.shape[2]
    lanes = near_ref.shape[2] + far_ref.shape[2]
    first = pl.program_id(0) * rows
    for row in range(rows):
        block = jnp.concatenate([near_ref[row], far_ref[row]], axis=1)
        lagged = pltpu.roll(block, (lanes - first - row) % lanes, 1)[:, :width]
        out_ref[row] = lagged * weight_ref[row : row + 1, :]


def band_of(near, far, weights, rows=8):
    own, lags, half_lanes = near.shape
    width = weights.shape[1]
    return pl.pallas_call(
        band_kernel,
        out_shape=jax.ShapeDtypeStruct((own, lags, width), jnp.float32),
        grid=(own // rows,),
        in_specs=[
            pl.BlockSpec((rows, lags, half_lanes), lambda i: (i, 0, 0)),
            pl.BlockSpec((rows, lags, half_lanes), lambda i: (i, 0, 0)),
            pl.BlockSpec((rows, width), lambda i: (i, 0)),
        ],
        out_specs=pl.BlockSpec((rows, lags, width), lambda i: (i, 0, 0)),
    )(near, far, weights)


def pack_kernel(raw_ref, out_ref, pad_ref):
    rows, width = raw_ref.shape[1], raw_ref.shape[2]
    half, lanes = out_ref.shape[1], out_ref.shape[2]
    pad_ref[...] = jnp.zeros(pad_ref.shape, jnp.float32)
    pad_ref[:rows] = raw_ref[0].astype(jnp.float32)
    top, bottom = pad_ref[:half], pad_ref[half:]
    low = lax.broadcasted_iota(jnp.int32, top.shape, 1) % lanes < lanes // 2
    even = jnp.where(low, top, pltpu.roll(bottom, lanes // 2, 1)).astype(out_ref.dtype)
    odd = jnp.where(low, pltpu.roll(top, width - lanes // 2, 1), bottom).astype(out_ref.dtype)
    for tile in range(out_ref.shape[0] // 2):
        out_ref[2 * tile] = even[:, tile * lanes : (tile + 1) * lanes]
        out_ref[2 * tile + 1] = odd[:, tile * lanes : (tile + 1) * lanes]


def pack(raw_strain, half, tiles_per_step=32):
    _, rows, channels = raw_strain.shape
    lanes = 128
    tiles = channels // lanes
    return pl.pallas_call(
        pack_kernel,
        out_shape=jax.ShapeDtypeStruct((2 * tiles, half, lanes), raw_strain.dtype),
        grid=(tiles // tiles_per_step,),
        in_specs=[pl.BlockSpec((1, rows, tiles_per_step * lanes), lambda i: (0, 0, i))],
        out_specs=pl.BlockSpec((2 * tiles_per_step, half, lanes), lambda i: (i, 0, 0)),
        scratch_shapes=[pltpu.VMEM((2 * half, tiles_per_step * lanes), jnp.float32)],
    )(raw_strain)


def local(raw_strain, window_valid, band_first, band_end):
    n_ch = lax.axis_size("ch")
    n_grp = lax.axis_size("grp")
    _, t_here, channels = raw_strain.shape
    per_dev = channels // n_ch
    pair_width = 2 * per_dev
    half = ((t_here + 1) // 2 + 15) // 16 * 16
    me = lax.axis_index("ch")
    side = me % 2

    samples = pack(raw_strain, half)
    samples, window_valid = lax.optimization_barrier((samples, window_valid))
    samples = lax.all_to_all(samples, "ch", 0, 0, tiled=True)
    samples = samples.reshape(n_ch, half, 2, per_dev)

    block_starts = jnp.arange(n_ch, dtype=jnp.int32) * t_here
    offsets = jnp.arange(2 * half, dtype=jnp.int32)
    table = dft_rows(block_starts, offsets, NT, F).reshape(n_ch, 2, half, 2 * F)
    spectra = jnp.einsum("srhc,shrf->cf", samples, table, preferred_element_type=jnp.float32)

    whitened = whiten(spectra, F, SMOOTH)
    valid_flags = window_valid.astype(jnp.bfloat16)
    group_index = lax.axis_index("grp")
    own_flags = lax.dynamic_slice_in_dim(valid_flags, group_index, 1, 0)
    whitened = whitened * own_flags[0][:, None]
    blocks_up = (KH + per_dev - 1) // per_dev
    own_rows = jnp.broadcast_to(whitened[None], (n_grp,) + whitened.shape)
    own_rows = lax.all_to_all(own_rows, "grp", 0, 0, tiled=True)
    white_parts = [own_rows]
    flag_parts = [valid_flags]
    for neighbour in range(1, blocks_up + 1):
        moved_white, moved_flags = from_behind((own_rows, valid_flags), "ch", -neighbour)
        white_parts.append(moved_white)
        flag_parts.append(moved_flags)
    rows_used = per_dev * (blocks_up + 1)
    lanes = 128 * pl.cdiv(rows_used, 128)
    white_parts.append(jnp.zeros((n_grp, lanes - rows_used, 2 * F), jnp.bfloat16))
    near = jnp.concatenate(white_parts[:2], axis=1)
    far = jnp.concatenate(white_parts[2:], axis=1)
    ext_flags = jnp.concatenate(flag_parts, axis=1)

    pair_full = jnp.einsum("na,nb->ab", valid_flags, ext_flags, preferred_element_type=jnp.float32)
    pair_counts = diagonal_band(pair_full, KH)
    turned = unturned(own_rows, -(LAGS // 2), LAGS, LAG_STEP, NT, F)
    near = jnp.einsum("walj,wbj->alb", turned, near, preferred_element_type=jnp.float32)
    far = jnp.einsum("walj,wbj->alb", turned, far, preferred_element_type=jnp.float32)
    weights = band_weights(pair_counts, band_first, band_end, F)
    return band_of(near, far, weights)


def solution(mesh):
    placed = (P("grp", "ch", None), P(None, "ch"), P("ch"), P("ch"))
    return jax.shard_map(
        local, mesh=mesh, in_specs=placed, out_specs=P("ch", None, None), check_vma=False
    )
```

```python
import jax
import jax.numpy as jnp
from jax import lax
from jax.experimental import pallas as pl
from jax.experimental.pallas import tpu as pltpu
from jax.sharding import PartitionSpec as P


NT = 7680
F = 384
KH = 128
SMOOTH = 65
LAGS = 32
LAG_STEP = 10


eps_white = 1e-06


def from_behind(array, axis, by):
    count = lax.axis_size(axis)
    pairs = [(i, i + by) for i in range(count) if 0 <= i + by < count]
    return lax.ppermute(array, axis, pairs)


def smoothing_matrix(bin_count, window_bins):
    row_index = jnp.arange(bin_count, dtype=jnp.int32)[:, None]
    col_index = jnp.arange(bin_count, dtype=jnp.int32)[None, :]
    distance = (row_index - col_index) % bin_count
    halfwidth = window_bins // 2
    inside = (distance <= halfwidth) | (distance >= bin_count - halfwidth)
    return inside.astype(jnp.float32)


def whiten(spectra, bin_count, window_bins):
    real_part = spectra[..., :bin_count]
    imag_part = spectra[..., bin_count:]
    magnitude = jnp.sqrt(real_part * real_part + imag_part * imag_part)
    averaged = (
        jnp.dot(
            magnitude,
            smoothing_matrix(bin_count, window_bins),
            precision=lax.Precision.HIGHEST,
            preferred_element_type=jnp.float32,
        )
        / window_bins
    )
    factor = 1.0 / (averaged + eps_white)
    return (spectra * jnp.concatenate([factor, factor], axis=-1)).astype(jnp.bfloat16)


def phase_of(index, samples):
    return (index % samples).astype(jnp.float32) * (2.0 * jnp.pi / samples)


def dft_rows(block_starts, offsets, samples, bin_count):
    orders = jnp.arange(1, bin_count + 1, dtype=jnp.int32)[None, :]
    outer = phase_of(block_starts[:, None] * orders, samples)
    inner = phase_of(offsets[:, None] * orders, samples)
    outer_cos, outer_sin = jnp.cos(outer)[:, None, :], jnp.sin(outer)[:, None, :]
    inner_cos, inner_sin = jnp.cos(inner)[None, :, :], jnp.sin(inner)[None, :, :]
    cosine = outer_cos * inner_cos - outer_sin * inner_sin
    sine_part = outer_sin * inner_cos + outer_cos * inner_sin
    table = jnp.concatenate([cosine, -sine_part], axis=-1)
    return table.reshape(-1, 2 * bin_count).astype(jnp.bfloat16)


def unturned(own, lag_first, lag_count, lag_step, samples, bin_count):
    orders = jnp.arange(1, bin_count + 1, dtype=jnp.int32)[None, :]
    shifts = ((lag_first + jnp.arange(lag_count, dtype=jnp.int32)) * lag_step)[:, None]
    phases = (shifts * orders % samples).astype(jnp.float32) * (2.0 * jnp.pi / samples)
    cosine = jnp.cos(phases)
    sine_part = jnp.sin(phases)
    real_part = own[..., :bin_count].astype(jnp.float32)[..., None, :]
    imag_part = own[..., bin_count:].astype(jnp.float32)[..., None, :]
    back_real = real_part * cosine - imag_part * sine_part
    back_imag = imag_part * cosine + real_part * sine_part
    return jnp.concatenate([back_real, back_imag], axis=-1).astype(jnp.bfloat16)


def diagonal_band(matrix, offsets):
    row_count, col_count = matrix.shape
    flat_rows = matrix.reshape(row_count * col_count)
    padded = jnp.concatenate([flat_rows, jnp.zeros((row_count,), matrix.dtype)])
    skewed = padded.reshape(row_count, col_count + 1)
    return skewed[:, :offsets]


def band_weights(pair_counts, band_lows, band_highs, bin_count):
    offsets = jnp.arange(pair_counts.shape[1], dtype=jnp.int32)[None, :]
    in_band = (offsets >= band_lows[:, None]) & (offsets < band_highs[:, None])
    return jnp.where(
        in_band, 1.0 / jnp.sqrt(float(bin_count) * jnp.maximum(pair_counts, 1.0)), 0.0
    )


def band_kernel(near_ref, far_ref, weight_ref, out_ref):
    width = out_ref.shape[2]
    lanes = near_ref.shape[2] + far_ref.shape[2]
    for row in range(out_ref.shape[0]):
        block = jnp.concatenate([near_ref[row], far_ref[row]], axis=1)
        lagged = pltpu.roll(block, (lanes - row) % lanes, 1)[:, :width]
        out_ref[row] = lagged * weight_ref[row : row + 1, :]


def band_of(near, far, weights):
    rows, lags, _ = near.shape
    width = weights.shape[1]
    return pl.pallas_call(
        band_kernel,
        out_shape=jax.ShapeDtypeStruct((rows, lags, width), jnp.float32),
        in_specs=[pl.BlockSpec(memory_space=pltpu.VMEM)] * 3,
        out_specs=pl.BlockSpec(memory_space=pltpu.VMEM),
    )(near, far, weights)


def pack_kernel(raw_ref, out_ref, pad_ref):
    rows, width = raw_ref.shape[1], raw_ref.shape[2]
    half, lanes = out_ref.shape[1], out_ref.shape[2]
    pad_ref[...] = jnp.zeros(pad_ref.shape, jnp.float32)
    pad_ref[:rows] = raw_ref[0].astype(jnp.float32)
    top, bottom = pad_ref[:half], pad_ref[half:]
    low = lax.broadcasted_iota(jnp.int32, top.shape, 1) % lanes < lanes // 2
    even = jnp.where(low, top, pltpu.roll(bottom, lanes // 2, 1)).astype(out_ref.dtype)
    odd = jnp.where(low, pltpu.roll(top, width - lanes // 2, 1), bottom).astype(out_ref.dtype)
    for tile in range(out_ref.shape[0] // 2):
        out_ref[2 * tile] = even[:, tile * lanes : (tile + 1) * lanes]
        out_ref[2 * tile + 1] = odd[:, tile * lanes : (tile + 1) * lanes]


def pack(raw_strain, half, tiles_per_step=32):
    _, rows, channels = raw_strain.shape
    lanes = 128
    tiles = channels // lanes
    return pl.pallas_call(
        pack_kernel,
        out_shape=jax.ShapeDtypeStruct((2 * tiles, half, lanes), raw_strain.dtype),
        grid=(tiles // tiles_per_step,),
        in_specs=[pl.BlockSpec((1, rows, tiles_per_step * lanes), lambda i: (0, 0, i))],
        out_specs=pl.BlockSpec((2 * tiles_per_step, half, lanes), lambda i: (i, 0, 0)),
        scratch_shapes=[pltpu.VMEM((2 * half, tiles_per_step * lanes), jnp.float32)],
    )(raw_strain)


def local(raw_strain, window_valid, band_first, band_end):
    n_ch = lax.axis_size("ch")
    n_grp = lax.axis_size("grp")
    _, t_here, channels = raw_strain.shape
    per_dev = channels // n_ch
    half = ((t_here + 1) // 2 + 15) // 16 * 16

    samples = pack(raw_strain, half)
    samples, window_valid = lax.optimization_barrier((samples, window_valid))
    samples = lax.all_to_all(samples, "ch", 0, 0, tiled=True)
    samples = samples.reshape(n_ch, half, 2, per_dev)

    block_starts = jnp.arange(n_ch, dtype=jnp.int32) * t_here
    offsets = jnp.arange(2 * half, dtype=jnp.int32)
    table = dft_rows(block_starts, offsets, NT, F).reshape(n_ch, 2, half, 2 * F)
    spectra = jnp.einsum("srhc,shrf->cf", samples, table, preferred_element_type=jnp.float32)

    whitened = whiten(spectra, F, SMOOTH)
    valid_flags = window_valid.astype(jnp.bfloat16)
    group_index = lax.axis_index("grp")
    own_flags = lax.dynamic_slice_in_dim(valid_flags, group_index, 1, 0)
    whitened = whitened * own_flags[0][:, None]
    blocks_up = (KH + per_dev - 1) // per_dev
    own_rows = jnp.broadcast_to(whitened[None], (n_grp,) + whitened.shape)
    own_rows = lax.all_to_all(own_rows, "grp", 0, 0, tiled=True)
    white_parts = [own_rows]
    flag_parts = [valid_flags]
    for neighbour in range(1, blocks_up + 1):
        white_parts.append(from_behind(own_rows, "ch", -neighbour))
        flag_parts.append(from_behind(valid_flags, "ch", -neighbour))
    rows_used = per_dev * (blocks_up + 1)
    lanes = 128 * pl.cdiv(rows_used, 128)
    white_parts.append(jnp.zeros((n_grp, lanes - rows_used, 2 * F), jnp.bfloat16))
    near = jnp.concatenate(white_parts[:2], axis=1)
    far = jnp.concatenate(white_parts[2:], axis=1)
    ext_flags = jnp.concatenate(flag_parts, axis=1)

    pair_full = jnp.einsum("na,nb->ab", valid_flags, ext_flags, preferred_element_type=jnp.float32)
    pair_counts = diagonal_band(pair_full, KH)
    turned = unturned(own_rows, -(LAGS // 2), LAGS, LAG_STEP, NT, F)
    near = jnp.einsum("walj,wbj->alb", turned, near, preferred_element_type=jnp.float32)
    far = jnp.einsum("walj,wbj->alb", turned, far, preferred_element_type=jnp.float32)
    weights = band_weights(pair_counts, band_first, band_end, F)
    return band_of(near, far, weights)


def solution(mesh):
    placed = (P("grp", "ch", None), P(None, "ch"), P("ch"), P("ch"))

    return jax.shard_map(
        local, mesh=mesh, in_specs=placed, out_specs=P("ch", None, None), check_vma=False
    )
```
